256 devices in a mesh: dp: 64 (over x, z, core), tensor: 4 (over y).
Axes of the slice: x: 4, y: 4, z: 8, core: 2. Of those that a mesh axis runs over, the one named last changes fastest.
Arguments:
- attention_grads: bfloat16 [64, 1, 512, 2048], P('dp', None, None, 'tensor')
- expert_grads: bfloat16 [64, 1, 2, 512, 4096], P('dp', None, None, None, 'tensor')
- routing_grads: bfloat16 [64, 4, 1, 36, 512], P('dp', 'tensor'), may hold values from -640 to 640
- attention_master: float32 [512, 2048], P('dp', 'tensor'), may hold values from -0.25 to 0.25
- attention_first: float32 [512, 2048], P('dp', 'tensor'), may hold values from -4 to 4
- attention_second: float32 [512, 2048], P('dp', 'tensor'), may hold values from 0.05 to 2
- expert_master: float32 [2, 512, 4096], P(None, 'dp', 'tensor'), may hold values from -0.25 to 0.25
- expert_first: float32 [2, 512, 4096], P(None, 'dp', 'tensor'), may hold values from -4 to 4
- expert_second: float32 [2, 512, 4096], P(None, 'dp', 'tensor'), may hold values from 0.05 to 2
- routing_master: float32 [36, 512], P(None, ('dp', 'tensor')), may hold values from -4 to 4
- routing_first: float32 [36, 512], P(None, ('dp', 'tensor')), may hold values from -4 to 4
- routing_second: float32 [36, 512], P(None, ('dp', 'tensor')), may hold values from 0.05 to 2
- step_count: int32 [1], replicated, may hold values from 1 to 1000
- learn_rate: float32 [1], replicated, may hold values from 0.05 to 0.3
- clip_level: float32 [1], replicated, may hold values from 0.5 to 2
Outputs:
- attention_renewed: float32 [512, 2048], P('dp', 'tensor')
- attention_momentum: float32 [512, 2048], P('dp', 'tensor')
- attention_variance: float32 [512, 2048], P('dp', 'tensor')
- attention_served: bfloat16 [512, 2048], P(None, 'tensor')
- expert_renewed: float32 [2, 512, 4096], P(None, 'dp', 'tensor')
- expert_momentum: float32 [2, 512, 4096], P(None, 'dp', 'tensor')
- expert_variance: float32 [2, 512, 4096], P(None, 'dp', 'tensor')
- expert_served: bfloat16 [2, 512, 4096], P(None, None, 'tensor')
- routing_renewed: float32 [36, 512], P(None, ('dp', 'tensor'))
- routing_momentum: float32 [36, 512], P(None, ('dp', 'tensor'))
- routing_variance: float32 [36, 512], P(None, ('dp', 'tensor'))
- routing_served: bfloat16 [36, 512], replicated
The draws below stay inside these ranges and needn't reach their ends.
Inputs may be any that keep to these rules, and one draw needn't show every extreme that they name: `step_count`: the number of optimizer steps taken, this one included.
All inputs are finite; a program needn't handle non-finite values.
Results may differ from the reference program's by a relative error of at most 0.0004.
Values may be sent and summed in bfloat16 or wider, within the bound.
No kernel may reach another device: no remote copies, remote signals or barrier semaphores. Data moves between devices by JAX's collectives and lax.ppermute only.
A program may use at most 64 MiB of HBM per device.

```python
import math
import jax
import jax.numpy as jnp
from jax import lax

D = 512
FF = 2048
EXPERTS = 32
MICRO = 1
EXP_WIN = 2
ROUTE_ROWS = 36
PARAMS = 5261312
N_DP = 64
N_TENSOR = 4


def rough_partials(key, shape):
    key_base, key_row, key_col = jax.random.split(key, 3)
    rows = shape[-2]
    cols = shape[-1]
    row_place = jnp.arange(rows, dtype=jnp.float32) / rows
    col_place = jnp.arange(cols, dtype=jnp.float32) / cols
    row_scale = jnp.power(10.0, row_place) * jnp.exp(jax.random.uniform(key_row, (rows,), jnp.float32, -0.5, 0.5))
    col_scale = jnp.power(3.0, col_place) * jnp.exp(jax.random.uniform(key_col, (cols,), jnp.float32, -0.7, 0.7))
    base = jax.random.normal(key_base, shape, jnp.float32)
    return base * row_scale[:, None] * col_scale[None, :]


def draw_attention_grads(key, part):
    shape = (N_DP, MICRO, D, 4 * D)
    return rough_partials(jax.random.fold_in(key, 11), shape).astype(jnp.bfloat16)


def draw_expert_grads(key, part):
    shape = (N_DP, MICRO, EXP_WIN, D, 2 * FF)
    return rough_partials(jax.random.fold_in(key, 23), shape).astype(jnp.bfloat16)


def strengthened(values, key, source, target, blocks, factor):
    owner, partner = [(jnp.arange(values.shape[position]) // (values.shape[position] // blocks)).reshape([-1 if axis == position else 1 for axis in range(values.ndim)]) for position in (source, target)]
    chosen = jax.random.permutation(key, blocks)[partner]
    strong = (owner == chosen) | (owner == (partner + blocks // 2) % blocks)
    return jnp.where(strong, factor * values, values)


def level_of(rng, dims, cuts, low, high):
    factor_of, own = 1.0, jax.random.fold_in(rng, 6)
    for dim, parts in cuts:
        draws = jnp.exp(jax.random.uniform(jax.random.fold_in(own, dim), (parts,), jnp.float32, low / len(cuts), high / len(cuts)))
        factor_of = factor_of * jnp.repeat(draws, dims[dim] // parts).reshape([-1 if axis == dim else 1 for axis in range(len(dims))])
    return factor_of


def centred(own_key, extent, width, limit, cuts=(), kind=jnp.bfloat16):
    values = width * jax.random.normal(own_key, extent, jnp.float32)
    if cuts:
        values = values * level_of(own_key, extent, cuts, -0.22, 0.18)
    return jnp.clip(values, -limit, limit).astype(kind)


def heavy_noise(rng, extent, deviation, bound, shards, heavy, kind=jnp.bfloat16):
    result = deviation * jax.random.normal(rng, extent, jnp.float32)
    if shards:
        result = result * level_of(rng, extent, shards, -0.22, 0.18)
    return jnp.clip(strengthened(result, jax.random.fold_in(rng, 3), *heavy), -bound, bound).astype(kind)


def setup_inputs(seed: int = 0) -> dict:
    keys = jax.random.split(jax.random.key(seed), 16)
    attention_grads = draw_attention_grads(jax.random.fold_in(keys[15], 71), 0)
    expert_grads = draw_expert_grads(jax.random.fold_in(keys[15], 71), 0)
    routing_grads = heavy_noise(keys[2], (N_DP, N_TENSOR, MICRO, ROUTE_ROWS, D), 40.0, 640.0, ((0, 64), (1, 4)), (0, 4, 64, 4.0))
    attention_master = centred(keys[3], (D, 4 * D), D ** -0.5, 0.25, ((0, 64), (1, 4)), jnp.float32)
    attention_first = centred(keys[4], (D, 4 * D), 0.5, 4.0, ((0, 64), (1, 4)), jnp.float32)
    attention_second = jnp.clip(jnp.exp(math.log(2.0) - 3.6888794 * jax.random.uniform(keys[5], (D, 4 * D), jnp.float32) ** level_of(keys[5], (D, 4 * D), ((0, 64), (1, 4)), -0.2, 0.2)), 0.05, 2.0)
    expert_master = centred(keys[6], (EXP_WIN, D, 2 * FF), D ** -0.5, 0.25, ((1, 64), (2, 4)), jnp.float32)
    expert_first = centred(keys[7], (EXP_WIN, D, 2 * FF), 0.5, 4.0, ((1, 64), (2, 4)), jnp.float32)
    expert_second = jnp.clip(jnp.exp(math.log(2.0) - 3.6888794 * jax.random.uniform(keys[8], (EXP_WIN, D, 2 * FF), jnp.float32) ** level_of(keys[8], (EXP_WIN, D, 2 * FF), ((1, 64), (2, 4)), -0.2, 0.2)), 0.05, 2.0)
    routing_master = centred(keys[9], (ROUTE_ROWS, D), 0.5, 4.0, ((1, 256),), jnp.float32)
    routing_first = centred(keys[10], (ROUTE_ROWS, D), 0.5, 4.0, ((1, 256),), jnp.float32)
    routing_second = jnp.clip(jnp.exp(math.log(2.0) - 3.6888794 * jax.random.uniform(keys[11], (ROUTE_ROWS, D), jnp.float32) ** level_of(keys[11], (ROUTE_ROWS, D), ((1, 256),), -0.2, 0.2)), 0.05, 2.0)
    step_count = jax.random.randint(keys[12], (1,), 1, 1001).astype(jnp.int32)
    learn_rate = jnp.clip(jnp.exp(jax.random.uniform(keys[13], (1,), jnp.float32, math.log(0.05), math.log(0.3))), 0.05, 0.3)
    clip_level = jnp.clip(jnp.exp(jax.random.uniform(keys[14], (1,), jnp.float32, math.log(0.5), math.log(2.0))), 0.5, 2.0)
    return {"attention_grads": attention_grads, "expert_grads": expert_grads, "routing_grads": routing_grads, "attention_master": attention_master, "attention_first": attention_first, "attention_second": attention_second, "expert_master": expert_master, "expert_first": expert_first, "expert_second": expert_second, "routing_master": routing_master, "routing_first": routing_first, "routing_second": routing_second, "step_count": step_count, "learn_rate": learn_rate, "clip_level": clip_level}


BETA_ONE = 0.9
BETA_TWO = 0.999
EPSILON = 1e-08
DECAY = 0.1

def accumulate(grads):

    def add_slice(total, block):
        return (total + lax.optimization_barrier(jnp.sum(block.astype(jnp.float32), axis=0)), None)
    start = jnp.zeros(grads.shape[2:], jnp.float32)
    total, unused = lax.scan(add_slice, start, grads)
    return total

def adam_update(grad_sum, master, first, second, clip, rate, first_fix, second_fix, mask):
    grad = clip * grad_sum
    momentum = BETA_ONE * first + (1.0 - BETA_ONE) * grad
    variance = BETA_TWO * second + (1.0 - BETA_TWO) * grad * grad
    update = momentum / first_fix / (jnp.sqrt(variance / second_fix) + EPSILON) + DECAY * mask * master
    renewed = master - rate * update
    return (renewed, momentum, variance, renewed.astype(jnp.bfloat16))

def reference(attention_grads, expert_grads, routing_grads, attention_master, attention_first, attention_second, expert_master, expert_first, expert_second, routing_master, routing_first, routing_second, step_count, learn_rate, clip_level):
    attention_sum = accumulate(attention_grads)
    expert_sum = accumulate(expert_grads)
    flat_routing = routing_grads.reshape((routing_grads.shape[0] * routing_grads.shape[1],) + routing_grads.shape[2:])
    routing_sum = accumulate(flat_routing)
    squares = jnp.sum(attention_sum * attention_sum) + jnp.sum(expert_sum * expert_sum) + jnp.sum(routing_sum * routing_sum)
    grad_norm = jnp.sqrt(squares)
    clip = jnp.minimum(1.0, clip_level[0] * jnp.sqrt(jnp.float32(PARAMS)) / (grad_norm + 1e-06))
    steps_done = step_count[0].astype(jnp.float32)
    first_fix = 1.0 - jnp.power(jnp.float32(BETA_ONE), steps_done)
    second_fix = 1.0 - jnp.power(jnp.float32(BETA_TWO), steps_done)
    rate = learn_rate[0]
    row_index = jnp.arange(ROUTE_ROWS, dtype=jnp.int32)
    routing_mask = (row_index < EXPERTS).astype(jnp.float32)[:, None]
    attention_out = adam_update(attention_sum, attention_master, attention_first, attention_second, clip, rate, first_fix, second_fix, jnp.float32(1.0))
    expert_out = adam_update(expert_sum, expert_master, expert_first, expert_second, clip, rate, first_fix, second_fix, jnp.float32(1.0))
    routing_out = adam_update(routing_sum, routing_master, routing_first, routing_second, clip, rate, first_fix, second_fix, routing_mask)
    return (attention_out[0], attention_out[1], attention_out[2], attention_out[3], expert_out[0], expert_out[1], expert_out[2], expert_out[3], routing_out[0], routing_out[1], routing_out[2], routing_out[3])
```

```python
import jax
import jax.numpy as jnp
from jax import lax
from jax.sharding import PartitionSpec as P

EXPERTS = 32
PARAMS = 5261312


BETA_ONE = 0.9
BETA_TWO = 0.999
EPSILON = 1e-08
DECAY = 0.1


def adam_update(grad_sum, master, first, second, clip, rate, first_fix, second_fix, mask):
    grad = clip * grad_sum
    momentum = BETA_ONE * first + (1.0 - BETA_ONE) * grad
    variance = BETA_TWO * second + (1.0 - BETA_TWO) * grad * grad
    update = (
        momentum / first_fix / (jnp.sqrt(variance / second_fix) + EPSILON) + DECAY * mask * master
    )
    renewed = master - rate * update
    return (renewed, momentum, variance, renewed.astype(jnp.bfloat16))


def local(
    attention_grads,
    expert_grads,
    routing_grads,
    attention_master,
    attention_first,
    attention_second,
    expert_master,
    expert_first,
    expert_second,
    routing_master,
    routing_first,
    routing_second,
    step_count,
    learn_rate,
    clip_level,
):
    n_dp = lax.axis_size("dp")
    n_t = lax.axis_size("tensor")
    t_idx = lax.axis_index("tensor")

    att = attention_grads[0, 0]
    exp = expert_grads[0, 0]
    rte = routing_grads[0, 0, 0]
    rows, cols = att.shape
    n_e, e_rows, e_cols = exp.shape
    n_r, r_cols = rte.shape
    ra = rows // n_dp
    re = e_rows // n_dp
    rc = r_cols // n_dp
    own = rc // n_t

    att_blocks = att.reshape(n_dp, ra * cols)
    exp_blocks = exp.reshape(n_e, n_dp, re, e_cols).transpose(1, 0, 2, 3).reshape(n_dp, -1)
    rte_blocks = rte.reshape(n_r, n_dp, rc).transpose(1, 0, 2).reshape(n_dp, -1)
    send = jnp.concatenate([att_blocks, exp_blocks, rte_blocks], axis=1)
    got = lax.all_to_all(send, "dp", 0, 0, tiled=True)
    total = jnp.sum(got.astype(jnp.float32), axis=0)
    n_att = ra * cols
    n_exp = n_e * re * e_cols
    attention_sum = total[:n_att].reshape(ra, cols)
    expert_sum = total[n_att : n_att + n_exp].reshape(n_e, re, e_cols)
    route_part = total[n_att + n_exp :].reshape(n_r, rc)

    local_squares = jnp.sum(attention_sum * attention_sum) + jnp.sum(expert_sum * expert_sum)
    slot = (jnp.arange(rc) // own == t_idx)[None, :]

    def placed(values):
        return jnp.where(slot, jnp.tile(values, (1, n_t)), 0.0)

    packed = jnp.stack(
        [
            route_part,
            placed(routing_master),
            placed(routing_first),
            placed(routing_second),
            jnp.full((n_r, rc), 0.0).at[0, 0].set(local_squares),
        ]
    )
    packed = lax.psum(packed, "tensor")
    route_sum = packed[0]
    route_master_blk, route_first_blk, route_second_blk = packed[1], packed[2], packed[3]
    group_squares = packed[4, 0, 0] + jnp.sum(route_sum * route_sum)

    spread = jnp.broadcast_to(group_squares, (n_dp, 1))
    squares = jnp.sum(lax.all_to_all(spread, "dp", 0, 0, tiled=True))

    grad_norm = jnp.sqrt(squares)
    clip = jnp.minimum(1.0, clip_level[0] * jnp.sqrt(jnp.float32(PARAMS)) / (grad_norm + 1e-06))
    steps_done = step_count[0].astype(jnp.float32)
    first_fix = 1.0 - jnp.power(jnp.float32(BETA_ONE), steps_done)
    second_fix = 1.0 - jnp.power(jnp.float32(BETA_TWO), steps_done)
    rate = learn_rate[0]
    one = jnp.float32(1.0)
    attention_out = adam_update(
        attention_sum, attention_master, attention_first, attention_second,
        clip, rate, first_fix, second_fix, one,
    )
    expert_out = adam_update(
        expert_sum, expert_master, expert_first, expert_second,
        clip, rate, first_fix, second_fix, one,
    )
    row_index = jnp.arange(n_r, dtype=jnp.int32)
    routing_mask = (row_index < EXPERTS).astype(jnp.float32)[:, None]
    routing_out = adam_update(
        route_sum, route_master_blk, route_first_blk, route_second_blk,
        clip, rate, first_fix, second_fix, routing_mask,
    )

    def mine(values):
        return lax.dynamic_slice_in_dim(values, t_idx * own, own, axis=1)

    served = jnp.concatenate(
        [
            attention_out[3].reshape(-1),
            expert_out[3].reshape(-1),
            routing_out[3].reshape(-1),
        ]
    )
    gathered = lax.all_to_all(jnp.broadcast_to(served, (n_dp,) + served.shape), "dp", 0, 0, tiled=True)
    attention_served = gathered[:, :n_att].reshape(rows, cols)
    expert_served = (
        gathered[:, n_att : n_att + n_exp]
        .reshape(n_dp, n_e, re, e_cols)
        .transpose(1, 0, 2, 3)
        .reshape(n_e, e_rows, e_cols)
    )
    routing_served = (
        gathered[:, n_att + n_exp :].reshape(n_dp, n_r, rc).transpose(1, 0, 2).reshape(n_r, r_cols)
    )
    return (
        attention_out[0],
        attention_out[1],
        attention_out[2],
        attention_served,
        expert_out[0],
        expert_out[1],
        expert_out[2],
        expert_served,
        mine(routing_out[0]),
        mine(routing_out[1]),
        mine(routing_out[2]),
        routing_served,
    )


def solution(mesh):
    in_specs = (
        P("dp", None, None, "tensor"),
        P("dp", None, None, None, "tensor"),
        P("dp", "tensor", None, None, None),
        P("dp", "tensor"),
        P("dp", "tensor"),
        P("dp", "tensor"),
        P(None, "dp", "tensor"),
        P(None, "dp", "tensor"),
        P(None, "dp", "tensor"),
        P(None, ("dp", "tensor")),
        P(None, ("dp", "tensor")),
        P(None, ("dp", "tensor")),
        P(),
        P(),
        P(),
    )
    out_specs = (
        P("dp", "tensor"),
        P("dp", "tensor"),
        P("dp", "tensor"),
        P(None, "tensor"),
        P(None, "dp", "tensor"),
        P(None, "dp", "tensor"),
        P(None, "dp", "tensor"),
        P(None, None, "tensor"),
        P(None, ("dp", "tensor")),
        P(None, ("dp", "tensor")),
        P(None, ("dp", "tensor")),
        P(),
    )
    return jax.shard_map(local, mesh=mesh, in_specs=in_specs, out_specs=out_specs, check_vma=False)
```

```python
import jax
import jax.numpy as jnp
from jax import lax
from jax.sharding import PartitionSpec as P

EXPERTS = 32
PARAMS = 5261312


BETA_ONE = 0.9
BETA_TWO = 0.999
EPSILON = 1e-08
DECAY = 0.1


def adam_update(grad_sum, master, first, second, clip, rate, first_fix, second_fix, mask):
    grad = clip * grad_sum
    momentum = BETA_ONE * first + (1.0 - BETA_ONE) * grad
    variance = BETA_TWO * second + (1.0 - BETA_TWO) * grad * grad
    update = (
        momentum / first_fix / (jnp.sqrt(variance / second_fix) + EPSILON) + DECAY * mask * master
    )
    renewed = master - rate * update
    return (renewed, momentum, variance, renewed.astype(jnp.bfloat16))


def local(
    attention_grads,
    expert_grads,
    routing_grads,
    attention_master,
    attention_first,
    attention_second,
    expert_master,
    expert_first,
    expert_second,
    routing_master,
    routing_first,
    routing_second,
    step_count,
    learn_rate,
    clip_level,
):
    n_dp = lax.axis_size("dp")
    n_t = lax.axis_size("tensor")
    t_idx = lax.axis_index("tensor")

    att = attention_grads[0, 0]
    exp = expert_grads[0, 0]
    rte = routing_grads[0, 0, 0]
    rows, cols = att.shape
    n_e, e_rows, e_cols = exp.shape
    n_r, r_cols = rte.shape
    ra = rows // n_dp
    re = e_rows // n_dp
    rc = r_cols // n_dp
    own = rc // n_t

    att_got = lax.all_to_all(att, "dp", 0, 0, tiled=True)
    exp_got = lax.all_to_all(exp, "dp", 1, 1, tiled=True)
    rte_got = lax.all_to_all(rte.T, "dp", 0, 0, tiled=True)
    attention_sum = jnp.sum(att_got.reshape(n_dp, ra, cols).astype(jnp.float32), axis=0)
    expert_sum = jnp.sum(exp_got.reshape(n_e, n_dp, re, e_cols).astype(jnp.float32), axis=1)
    route_part = jnp.sum(rte_got.reshape(n_dp, rc, n_r).astype(jnp.float32), axis=0).T

    local_squares = jnp.sum(attention_sum * attention_sum) + jnp.sum(expert_sum * expert_sum)
    slot = (jnp.arange(rc) // own == t_idx)[None, :]

    def placed(values):
        return jnp.where(slot, jnp.tile(values, (1, n_t)), 0.0)

    packed = jnp.stack(
        [
            route_part,
            placed(routing_master),
            placed(routing_first),
            placed(routing_second),
            jnp.full((n_r, rc), 0.0).at[0, 0].set(local_squares),
        ]
    )
    packed = lax.psum(packed, "tensor")
    route_sum = packed[0]
    route_master_blk, route_first_blk, route_second_blk = packed[1], packed[2], packed[3]
    group_squares = packed[4, 0, 0] + jnp.sum(route_sum * route_sum)

    spread = jnp.broadcast_to(group_squares, (n_dp, 1))
    squares = jnp.sum(lax.all_to_all(spread, "dp", 0, 0, tiled=True))

    grad_norm = jnp.sqrt(squares)
    clip = jnp.minimum(1.0, clip_level[0] * jnp.sqrt(jnp.float32(PARAMS)) / (grad_norm + 1e-06))
    steps_done = step_count[0].astype(jnp.float32)
    first_fix = 1.0 - jnp.power(jnp.float32(BETA_ONE), steps_done)
    second_fix = 1.0 - jnp.power(jnp.float32(BETA_TWO), steps_done)
    rate = learn_rate[0]
    one = jnp.float32(1.0)
    attention_out = adam_update(
        attention_sum, attention_master, attention_first, attention_second,
        clip, rate, first_fix, second_fix, one,
    )
    expert_out = adam_update(
        expert_sum, expert_master, expert_first, expert_second,
        clip, rate, first_fix, second_fix, one,
    )
    row_index = jnp.arange(n_r, dtype=jnp.int32)
    routing_mask = (row_index < EXPERTS).astype(jnp.float32)[:, None]
    routing_out = adam_update(
        route_sum, route_master_blk, route_first_blk, route_second_blk,
        clip, rate, first_fix, second_fix, routing_mask,
    )

    def mine(values):
        return lax.dynamic_slice_in_dim(values, t_idx * own, own, axis=1)

    att_srv = attention_out[3]
    exp_srv = expert_out[3]
    rte_srv = routing_out[3]
    attention_served = lax.all_to_all(
        jnp.broadcast_to(att_srv[None], (n_dp,) + att_srv.shape).reshape(rows, cols),
        "dp", 0, 0, tiled=True,
    )
    expert_served = lax.all_to_all(
        jnp.broadcast_to(exp_srv[:, None], (n_e, n_dp, re, e_cols)).reshape(n_e, e_rows, e_cols),
        "dp", 1, 1, tiled=True,
    )
    routing_served = lax.all_to_all(
        jnp.broadcast_to(rte_srv[:, None], (n_r, n_dp, rc)).reshape(n_r, r_cols),
        "dp", 1, 1, tiled=True,
    )
    return (
        attention_out[0],
        attention_out[1],
        attention_out[2],
        attention_served,
        expert_out[0],
        expert_out[1],
        expert_out[2],
        expert_served,
        mine(routing_out[0]),
        mine(routing_out[1]),
        mine(routing_out[2]),
        routing_served,
    )


def solution(mesh):
    in_specs = (
        P("dp", None, None, "tensor"),
        P("dp", None, None, None, "tensor"),
        P("dp", "tensor", None, None, None),
        P("dp", "tensor"),
        P("dp", "tensor"),
        P("dp", "tensor"),
        P(None, "dp", "tensor"),
        P(None, "dp", "tensor"),
        P(None, "dp", "tensor"),
        P(None, ("dp", "tensor")),
        P(None, ("dp", "tensor")),
        P(None, ("dp", "tensor")),
        P(),
        P(),
        P(),
    )
    out_specs = (
        P("dp", "tensor"),
        P("dp", "tensor"),
        P("dp", "tensor"),
        P(None, "tensor"),
        P(None, "dp", "tensor"),
        P(None, "dp", "tensor"),
        P(None, "dp", "tensor"),
        P(None, None, "tensor"),
        P(None, ("dp", "tensor")),
        P(None, ("dp", "tensor")),
        P(None, ("dp", "tensor")),
        P(),
    )
    return jax.shard_map(local, mesh=mesh, in_specs=in_specs, out_specs=out_specs, check_vma=False)
```

```python
import jax
import jax.numpy as jnp
from jax import lax
from jax.sharding import PartitionSpec as P

EXPERTS = 32
PARAMS = 5261312


BETA_ONE = 0.9
BETA_TWO = 0.999
EPSILON = 1e-08
DECAY = 0.1


def adam_update(grad_sum, master, first, second, clip, rate, first_fix, second_fix, mask):
    grad = clip * grad_sum
    momentum = BETA_ONE * first + (1.0 - BETA_ONE) * grad
    variance = BETA_TWO * second + (1.0 - BETA_TWO) * grad * grad
    update = (
        momentum / first_fix / (jnp.sqrt(variance / second_fix) + EPSILON) + DECAY * mask * master
    )
    renewed = master - rate * update
    return (renewed, momentum, variance, renewed.astype(jnp.bfloat16))


def local(
    attention_grads,
    expert_grads,
    routing_grads,
    attention_master,
    attention_first,
    attention_second,
    expert_master,
    expert_first,
    expert_second,
    routing_master,
    routing_first,
    routing_second,
    step_count,
    learn_rate,
    clip_level,
):
    n_dp = lax.axis_size("dp")
    n_t = lax.axis_size("tensor")
    t_idx = lax.axis_index("tensor")

    att = attention_grads[0, 0]
    exp = expert_grads[0, 0]
    rte = routing_grads[0, 0, 0]
    rows, cols = att.shape
    n_e, e_rows, e_cols = exp.shape
    n_r, r_cols = rte.shape
    ra = rows // n_dp
    re = e_rows // n_dp
    rc = r_cols // n_dp
    own = rc // n_t

    exp_rows = exp.transpose(1, 0, 2).reshape(e_rows, n_e * e_cols)
    send = jnp.concatenate([att, exp_rows, rte.T], axis=1)
    got = lax.all_to_all(send, "dp", 0, 0, tiled=True)
    total = jnp.sum(got.reshape(n_dp, ra, -1).astype(jnp.float32), axis=0)
    attention_sum = total[:, :cols]
    expert_sum = total[:, cols : cols + n_e * e_cols].reshape(re, n_e, e_cols).transpose(1, 0, 2)
    route_part = total[:, cols + n_e * e_cols :].T

    local_squares = jnp.sum(attention_sum * attention_sum) + jnp.sum(expert_sum * expert_sum)
    slot = (jnp.arange(rc) // own == t_idx)[None, :]

    def placed(values):
        return jnp.where(slot, jnp.tile(values, (1, n_t)), 0.0)

    packed = jnp.stack(
        [
            route_part,
            placed(routing_master),
            placed(routing_first),
            placed(routing_second),
            jnp.full((n_r, rc), 0.0).at[0, 0].set(local_squares),
        ]
    )
    packed = lax.psum(packed, "tensor")
    route_sum = packed[0]
    route_master_blk, route_first_blk, route_second_blk = packed[1], packed[2], packed[3]
    group_squares = packed[4, 0, 0] + jnp.sum(route_sum * route_sum)

    spread = jnp.broadcast_to(group_squares, (n_dp, 1))
    squares = jnp.sum(lax.all_to_all(spread, "dp", 0, 0, tiled=True))

    grad_norm = jnp.sqrt(squares)
    clip = jnp.minimum(1.0, clip_level[0] * jnp.sqrt(jnp.float32(PARAMS)) / (grad_norm + 1e-06))
    steps_done = step_count[0].astype(jnp.float32)
    first_fix = 1.0 - jnp.power(jnp.float32(BETA_ONE), steps_done)
    second_fix = 1.0 - jnp.power(jnp.float32(BETA_TWO), steps_done)
    rate = learn_rate[0]
    one = jnp.float32(1.0)
    attention_out = adam_update(
        attention_sum, attention_master, attention_first, attention_second,
        clip, rate, first_fix, second_fix, one,
    )
    expert_out = adam_update(
        expert_sum, expert_master, expert_first, expert_second,
        clip, rate, first_fix, second_fix, one,
    )
    row_index = jnp.arange(n_r, dtype=jnp.int32)
    routing_mask = (row_index < EXPERTS).astype(jnp.float32)[:, None]
    routing_out = adam_update(
        route_sum, route_master_blk, route_first_blk, route_second_blk,
        clip, rate, first_fix, second_fix, routing_mask,
    )

    def mine(values):
        return lax.dynamic_slice_in_dim(values, t_idx * own, own, axis=1)

    rest = jnp.concatenate([attention_out[3], routing_out[3].T], axis=1)
    rest = lax.all_gather(rest, "dp", axis=0, tiled=True)
    expert_served = lax.all_gather(expert_out[3], "dp", axis=1, tiled=True)
    attention_served = rest[:, :cols]
    routing_served = rest[:, cols:].T
    return (
        attention_out[0],
        attention_out[1],
        attention_out[2],
        attention_served,
        expert_out[0],
        expert_out[1],
        expert_out[2],
        expert_served,
        mine(routing_out[0]),
        mine(routing_out[1]),
        mine(routing_out[2]),
        routing_served,
    )


def solution(mesh):
    in_specs = (
        P("dp", None, None, "tensor"),
        P("dp", None, None, None, "tensor"),
        P("dp", "tensor", None, None, None),
        P("dp", "tensor"),
        P("dp", "tensor"),
        P("dp", "tensor"),
        P(None, "dp", "tensor"),
        P(None, "dp", "tensor"),
        P(None, "dp", "tensor"),
        P(None, ("dp", "tensor")),
        P(None, ("dp", "tensor")),
        P(None, ("dp", "tensor")),
        P(),
        P(),
        P(),
    )
    out_specs = (
        P("dp", "tensor"),
        P("dp", "tensor"),
        P("dp", "tensor"),
        P(None, "tensor"),
        P(None, "dp", "tensor"),
        P(None, "dp", "tensor"),
        P(None, "dp", "tensor"),
        P(None, None, "tensor"),
        P(None, ("dp", "tensor")),
        P(None, ("dp", "tensor")),
        P(None, ("dp", "tensor")),
        P(),
    )
    return jax.shard_map(local, mesh=mesh, in_specs=in_specs, out_specs=out_specs, check_vma=False)
```

```python
import jax
import jax.numpy as jnp
from jax import lax
from jax.sharding import Mesh, PartitionSpec as P

EXPERTS = 32
PARAMS = 5261312


BETA_ONE = 0.9
BETA_TWO = 0.999
EPSILON = 1e-08
DECAY = 0.1

DP_PARTS = ("dp_x", "dp_z", "dp_core")
DP = DP_PARTS


def adam_update(grad_sum, master, first, second, clip, rate, first_fix, second_fix, mask):
    grad = clip * grad_sum
    momentum = BETA_ONE * first + (1.0 - BETA_ONE) * grad
    variance = BETA_TWO * second + (1.0 - BETA_TWO) * grad * grad
    update = (
        momentum / first_fix / (jnp.sqrt(variance / second_fix) + EPSILON) + DECAY * mask * master
    )
    renewed = master - rate * update
    return (renewed, momentum, variance, renewed.astype(jnp.bfloat16))


def local(
    attention_grads,
    expert_grads,
    routing_grads,
    attention_master,
    attention_first,
    attention_second,
    expert_master,
    expert_first,
    expert_second,
    routing_master,
    routing_first,
    routing_second,
    step_count,
    learn_rate,
    clip_level,
):
    n_dp = lax.axis_size(DP)
    n_t = lax.axis_size("tensor")
    t_idx = lax.axis_index("tensor")

    att = attention_grads[0, 0]
    exp = expert_grads[0, 0]
    rte = routing_grads[0, 0, 0]
    rows, cols = att.shape
    n_e, e_rows, e_cols = exp.shape
    n_r, r_cols = rte.shape
    ra = rows // n_dp
    re = e_rows // n_dp
    rc = r_cols // n_dp
    own = rc // n_t

    exp_rows = exp.transpose(1, 0, 2).reshape(e_rows, n_e * e_cols)
    send = jnp.concatenate([att, exp_rows, rte.T], axis=1)
    got = lax.all_to_all(send, DP, 0, 0, tiled=True)
    total = jnp.sum(got.reshape(n_dp, ra, -1).astype(jnp.float32), axis=0)
    attention_sum = total[:, :cols]
    expert_sum = total[:, cols : cols + n_e * e_cols].reshape(re, n_e, e_cols).transpose(1, 0, 2)
    route_part = total[:, cols + n_e * e_cols :].T

    local_squares = jnp.sum(attention_sum * attention_sum) + jnp.sum(expert_sum * expert_sum)
    slot = (jnp.arange(rc) // own == t_idx)[None, :]

    def placed(values):
        return jnp.where(slot, jnp.tile(values, (1, n_t)), 0.0)

    packed = jnp.stack(
        [
            route_part,
            placed(routing_master),
            placed(routing_first),
            placed(routing_second),
            jnp.full((n_r, rc), 0.0).at[0, 0].set(local_squares),
        ]
    )
    packed = lax.psum(packed, "tensor")
    route_sum = packed[0]
    route_master_blk, route_first_blk, route_second_blk = packed[1], packed[2], packed[3]
    group_squares = packed[4, 0, 0] + jnp.sum(route_sum * route_sum)

    spread = jnp.broadcast_to(group_squares, (n_dp, 1))
    squares = jnp.sum(lax.all_to_all(spread, DP, 0, 0, tiled=True))

    grad_norm = jnp.sqrt(squares)
    clip = jnp.minimum(1.0, clip_level[0] * jnp.sqrt(jnp.float32(PARAMS)) / (grad_norm + 1e-06))
    steps_done = step_count[0].astype(jnp.float32)
    first_fix = 1.0 - jnp.power(jnp.float32(BETA_ONE), steps_done)
    second_fix = 1.0 - jnp.power(jnp.float32(BETA_TWO), steps_done)
    rate = learn_rate[0]
    one = jnp.float32(1.0)
    attention_out = adam_update(
        attention_sum, attention_master, attention_first, attention_second,
        clip, rate, first_fix, second_fix, one,
    )
    expert_out = adam_update(
        expert_sum, expert_master, expert_first, expert_second,
        clip, rate, first_fix, second_fix, one,
    )
    row_index = jnp.arange(n_r, dtype=jnp.int32)
    routing_mask = (row_index < EXPERTS).astype(jnp.float32)[:, None]
    routing_out = adam_update(
        route_sum, route_master_blk, route_first_blk, route_second_blk,
        clip, rate, first_fix, second_fix, routing_mask,
    )

    def mine(values):
        return lax.dynamic_slice_in_dim(values, t_idx * own, own, axis=1)

    def gather(values, axis):
        for name in reversed(DP_PARTS):
            values = lax.all_gather(values, name, axis=axis, tiled=True)
        return values

    rest = gather(jnp.concatenate([attention_out[3], routing_out[3].T], axis=1), 0)
    expert_served = gather(expert_out[3], 1)
    attention_served = rest[:, :cols]
    routing_served = rest[:, cols:].T
    return (
        attention_out[0],
        attention_out[1],
        attention_out[2],
        attention_served,
        expert_out[0],
        expert_out[1],
        expert_out[2],
        expert_served,
        mine(routing_out[0]),
        mine(routing_out[1]),
        mine(routing_out[2]),
        routing_served,
    )


def split_mesh(mesh):
    column = mesh.devices[:, 0]
    sizes = (
        len({d.coords[0] for d in column}),
        len({d.coords[2] for d in column}),
        len({d.core_on_chip for d in column}),
    )
    devices = mesh.devices.reshape(sizes + mesh.devices.shape[1:])
    return Mesh(devices, DP_PARTS + ("tensor",))


def solution(mesh):
    mesh = split_mesh(mesh)
    in_specs = (
        P(DP, None, None, "tensor"),
        P(DP, None, None, None, "tensor"),
        P(DP, "tensor", None, None, None),
        P(DP, "tensor"),
        P(DP, "tensor"),
        P(DP, "tensor"),
        P(None, DP, "tensor"),
        P(None, DP, "tensor"),
        P(None, DP, "tensor"),
        P(None, (DP + ("tensor",))),
        P(None, (DP + ("tensor",))),
        P(None, (DP + ("tensor",))),
        P(),
        P(),
        P(),
    )
    out_specs = (
        P(DP, "tensor"),
        P(DP, "tensor"),
        P(DP, "tensor"),
        P(None, "tensor"),
        P(None, DP, "tensor"),
        P(None, DP, "tensor"),
        P(None, DP, "tensor"),
        P(None, None, "tensor"),
        P(None, (DP + ("tensor",))),
        P(None, (DP + ("tensor",))),
        P(None, (DP + ("tensor",))),
        P(),
    )
    return jax.shard_map(local, mesh=mesh, in_specs=in_specs, out_specs=out_specs, check_vma=False)
```

```python
import jax
import jax.numpy as jnp
from jax import lax
from jax.sharding import Mesh, PartitionSpec as P

EXPERTS = 32
PARAMS = 5261312


BETA_ONE = 0.9
BETA_TWO = 0.999
EPSILON = 1e-08
DECAY = 0.1

DP_PARTS = ("dp_x", "dp_z", "dp_core")
DP = DP_PARTS


def adam_update(grad_sum, master, first, second, clip, rate, first_fix, second_fix, mask):
    grad = clip * grad_sum
    momentum = BETA_ONE * first + (1.0 - BETA_ONE) * grad
    variance = BETA_TWO * second + (1.0 - BETA_TWO) * grad * grad
    update = (
        momentum / first_fix / (jnp.sqrt(variance / second_fix) + EPSILON) + DECAY * mask * master
    )
    renewed = master - rate * update
    return (renewed, momentum, variance, renewed.astype(jnp.bfloat16))


def local(
    attention_grads,
    expert_grads,
    routing_grads,
    attention_master,
    attention_first,
    attention_second,
    expert_master,
    expert_first,
    expert_second,
    routing_master,
    routing_first,
    routing_second,
    step_count,
    learn_rate,
    clip_level,
):
    n_dp = lax.axis_size(DP)
    n_t = lax.axis_size("tensor")
    t_idx = lax.axis_index("tensor")

    att = attention_grads[0, 0]
    exp = expert_grads[0, 0]
    rte = routing_grads[0, 0, 0]
    rows, cols = att.shape
    n_e, e_rows, e_cols = exp.shape
    n_r, r_cols = rte.shape
    ra = rows // n_dp
    re = e_rows // n_dp
    rc = r_cols // n_dp
    own = rc // n_t

    exp_rows = exp.transpose(1, 0, 2).reshape(e_rows, n_e * e_cols)
    send = jnp.concatenate([att, exp_rows, rte.T], axis=1)
    got = lax.all_to_all(send, DP, 0, 0, tiled=True)
    total = jnp.sum(got.reshape(n_dp, ra, -1).astype(jnp.float32), axis=0)
    attention_sum = total[:, :cols]
    expert_sum = total[:, cols : cols + n_e * e_cols].reshape(re, n_e, e_cols).transpose(1, 0, 2)
    route_part = total[:, cols + n_e * e_cols :].T

    local_squares = jnp.sum(attention_sum * attention_sum) + jnp.sum(expert_sum * expert_sum)
    slot = (jnp.arange(rc) // own == t_idx)[None, :]

    def placed(values):
        return jnp.where(slot, jnp.tile(values, (1, n_t)), 0.0)

    packed = jnp.stack(
        [
            route_part,
            placed(routing_master),
            placed(routing_first),
            placed(routing_second),
            jnp.full((n_r, rc), 0.0).at[0, 0].set(local_squares),
        ]
    )
    packed = lax.psum(packed, "tensor")
    route_sum = packed[0]
    route_master_blk, route_first_blk, route_second_blk = packed[1], packed[2], packed[3]
    group_squares = packed[4, 0, 0] + jnp.sum(route_sum * route_sum)

    spread = jnp.broadcast_to(group_squares, (n_dp, 1))
    squares = jnp.sum(lax.all_to_all(spread, DP, 0, 0, tiled=True))

    grad_norm = jnp.sqrt(squares)
    clip = jnp.minimum(1.0, clip_level[0] * jnp.sqrt(jnp.float32(PARAMS)) / (grad_norm + 1e-06))
    steps_done = step_count[0].astype(jnp.float32)
    first_fix = 1.0 - jnp.power(jnp.float32(BETA_ONE), steps_done)
    second_fix = 1.0 - jnp.power(jnp.float32(BETA_TWO), steps_done)
    rate = learn_rate[0]
    one = jnp.float32(1.0)
    attention_out = adam_update(
        attention_sum, attention_master, attention_first, attention_second,
        clip, rate, first_fix, second_fix, one,
    )
    expert_out = adam_update(
        expert_sum, expert_master, expert_first, expert_second,
        clip, rate, first_fix, second_fix, one,
    )
    row_index = jnp.arange(n_r, dtype=jnp.int32)
    routing_mask = (row_index < EXPERTS).astype(jnp.float32)[:, None]
    routing_out = adam_update(
        route_sum, route_master_blk, route_first_blk, route_second_blk,
        clip, rate, first_fix, second_fix, routing_mask,
    )

    def mine(values):
        return lax.dynamic_slice_in_dim(values, t_idx * own, own, axis=1)

    def gather(values, axis):
        for name in reversed(DP_PARTS):
            values = lax.all_gather(values, name, axis=axis, tiled=True)
        return values

    rest = jnp.concatenate(
        [
            attention_out[3],
            expert_out[3].transpose(1, 0, 2).reshape(re, n_e * e_cols),
            routing_out[3].T,
        ],
        axis=1,
    )
    rest = gather(rest, 0)
    attention_served = rest[:, :cols]
    expert_served = (
        rest[:, cols : cols + n_e * e_cols].reshape(e_rows, n_e, e_cols).transpose(1, 0, 2)
    )
    routing_served = rest[:, cols + n_e * e_cols :].T
    return (
        attention_out[0],
        attention_out[1],
        attention_out[2],
        attention_served,
        expert_out[0],
        expert_out[1],
        expert_out[2],
        expert_served,
        mine(routing_out[0]),
        mine(routing_out[1]),
        mine(routing_out[2]),
        routing_served,
    )


def split_mesh(mesh):
    column = mesh.devices[:, 0]
    sizes = (
        len({d.coords[0] for d in column}),
        len({d.coords[2] for d in column}),
        len({d.core_on_chip for d in column}),
    )
    devices = mesh.devices.reshape(sizes + mesh.devices.shape[1:])
    return Mesh(devices, DP_PARTS + ("tensor",))


def solution(mesh):
    mesh = split_mesh(mesh)
    in_specs = (
        P(DP, None, None, "tensor"),
        P(DP, None, None, None, "tensor"),
        P(DP, "tensor", None, None, None),
        P(DP, "tensor"),
        P(DP, "tensor"),
        P(DP, "tensor"),
        P(None, DP, "tensor"),
        P(None, DP, "tensor"),
        P(None, DP, "tensor"),
        P(None, (DP + ("tensor",))),
        P(None, (DP + ("tensor",))),
        P(None, (DP + ("tensor",))),
        P(),
        P(),
        P(),
    )
    out_specs = (
        P(DP, "tensor"),
        P(DP, "tensor"),
        P(DP, "tensor"),
        P(None, "tensor"),
        P(None, DP, "tensor"),
        P(None, DP, "tensor"),
        P(None, DP, "tensor"),
        P(None, None, "tensor"),
        P(None, (DP + ("tensor",))),
        P(None, (DP + ("tensor",))),
        P(None, (DP + ("tensor",))),
        P(),
    )
    return jax.shard_map(local, mesh=mesh, in_specs=in_specs, out_specs=out_specs, check_vma=False)
```

```python
import jax
import jax.numpy as jnp
from jax import lax
from jax.sharding import Mesh, PartitionSpec as P

EXPERTS = 32
PARAMS = 5261312


BETA_ONE = 0.9
BETA_TWO = 0.999
EPSILON = 1e-08
DECAY = 0.1

DP_PARTS = ("dp_x", "dp_z", "dp_core")
DP = DP_PARTS


def adam_update(grad_sum, master, first, second, clip, rate, first_fix, second_fix, mask):
    grad = clip * grad_sum
    momentum = BETA_ONE * first + (1.0 - BETA_ONE) * grad
    variance = BETA_TWO * second + (1.0 - BETA_TWO) * grad * grad
    update = (
        momentum / first_fix / (jnp.sqrt(variance / second_fix) + EPSILON) + DECAY * mask * master
    )
    renewed = master - rate * update
    return (renewed, momentum, variance, renewed.astype(jnp.bfloat16))


def local(
    attention_grads,
    expert_grads,
    routing_grads,
    attention_master,
    attention_first,
    attention_second,
    expert_master,
    expert_first,
    expert_second,
    routing_master,
    routing_first,
    routing_second,
    step_count,
    learn_rate,
    clip_level,
):
    n_dp = lax.axis_size(DP)
    n_t = lax.axis_size("tensor")
    t_idx = lax.axis_index("tensor")

    att = attention_grads[0, 0]
    exp = expert_grads[0, 0]
    rte = routing_grads[0, 0, 0]
    rows, cols = att.shape
    n_e, e_rows, e_cols = exp.shape
    n_r, r_cols = rte.shape
    ra = rows // n_dp
    re = e_rows // n_dp
    rc = r_cols // n_dp
    own = rc // n_t

    send = jnp.concatenate([att, rte.T], axis=1)
    got = lax.all_to_all(send, DP, 0, 0, tiled=True)
    exp_got = lax.all_to_all(exp, DP, 1, 1, tiled=True)
    total = jnp.sum(got.reshape(n_dp, ra, -1).astype(jnp.float32), axis=0)
    attention_sum = total[:, :cols]
    route_part = total[:, cols:].T
    expert_sum = jnp.sum(exp_got.reshape(n_e, n_dp, re, e_cols).astype(jnp.float32), axis=1)

    local_squares = jnp.sum(attention_sum * attention_sum) + jnp.sum(expert_sum * expert_sum)
    slot = (jnp.arange(rc) // own == t_idx)[None, :]

    def placed(values):
        return jnp.where(slot, jnp.tile(values, (1, n_t)), 0.0)

    packed = jnp.stack(
        [
            route_part,
            placed(routing_master),
            placed(routing_first),
            placed(routing_second),
            jnp.full((n_r, rc), 0.0).at[0, 0].set(local_squares),
        ]
    )
    packed = lax.psum(packed, "tensor")
    route_sum = packed[0]
    route_master_blk, route_first_blk, route_second_blk = packed[1], packed[2], packed[3]
    group_squares = packed[4, 0, 0] + jnp.sum(route_sum * route_sum)

    spread = jnp.broadcast_to(group_squares, (n_dp, 1))
    squares = jnp.sum(lax.all_to_all(spread, DP, 0, 0, tiled=True))

    grad_norm = jnp.sqrt(squares)
    clip = jnp.minimum(1.0, clip_level[0] * jnp.sqrt(jnp.float32(PARAMS)) / (grad_norm + 1e-06))
    steps_done = step_count[0].astype(jnp.float32)
    first_fix = 1.0 - jnp.power(jnp.float32(BETA_ONE), steps_done)
    second_fix = 1.0 - jnp.power(jnp.float32(BETA_TWO), steps_done)
    rate = learn_rate[0]
    one = jnp.float32(1.0)
    attention_out = adam_update(
        attention_sum, attention_master, attention_first, attention_second,
        clip, rate, first_fix, second_fix, one,
    )
    expert_out = adam_update(
        expert_sum, expert_master, expert_first, expert_second,
        clip, rate, first_fix, second_fix, one,
    )
    row_index = jnp.arange(n_r, dtype=jnp.int32)
    routing_mask = (row_index < EXPERTS).astype(jnp.float32)[:, None]
    routing_out = adam_update(
        route_sum, route_master_blk, route_first_blk, route_second_blk,
        clip, rate, first_fix, second_fix, routing_mask,
    )

    def mine(values):
        return lax.dynamic_slice_in_dim(values, t_idx * own, own, axis=1)

    def gather(values, axis):
        for name in reversed(DP_PARTS):
            values = lax.all_gather(values, name, axis=axis, tiled=True)
        return values

    rest = jnp.concatenate(
        [
            attention_out[3],
            expert_out[3].transpose(1, 0, 2).reshape(re, n_e * e_cols),
            routing_out[3].T,
        ],
        axis=1,
    )
    rest = gather(rest, 0)
    attention_served = rest[:, :cols]
    expert_served = (
        rest[:, cols : cols + n_e * e_cols].reshape(e_rows, n_e, e_cols).transpose(1, 0, 2)
    )
    routing_served = rest[:, cols + n_e * e_cols :].T
    return (
        attention_out[0],
        attention_out[1],
        attention_out[2],
        attention_served,
        expert_out[0],
        expert_out[1],
        expert_out[2],
        expert_served,
        mine(routing_out[0]),
        mine(routing_out[1]),
        mine(routing_out[2]),
        routing_served,
    )


def split_mesh(mesh):
    column = mesh.devices[:, 0]
    sizes = (
        len({d.coords[0] for d in column}),
        len({d.coords[2] for d in column}),
        len({d.core_on_chip for d in column}),
    )
    devices = mesh.devices.reshape(sizes + mesh.devices.shape[1:])
    return Mesh(devices, DP_PARTS + ("tensor",))


def solution(mesh):
    mesh = split_mesh(mesh)
    in_specs = (
        P(DP, None, None, "tensor"),
        P(DP, None, None, None, "tensor"),
        P(DP, "tensor", None, None, None),
        P(DP, "tensor"),
        P(DP, "tensor"),
        P(DP, "tensor"),
        P(None, DP, "tensor"),
        P(None, DP, "tensor"),
        P(None, DP, "tensor"),
        P(None, (DP + ("tensor",))),
        P(None, (DP + ("tensor",))),
        P(None, (DP + ("tensor",))),
        P(),
        P(),
        P(),
    )
    out_specs = (
        P(DP, "tensor"),
        P(DP, "tensor"),
        P(DP, "tensor"),
        P(None, "tensor"),
        P(None, DP, "tensor"),
        P(None, DP, "tensor"),
        P(None, DP, "tensor"),
        P(None, None, "tensor"),
        P(None, (DP + ("tensor",))),
        P(None, (DP + ("tensor",))),
        P(None, (DP + ("tensor",))),
        P(),
    )
    return jax.shard_map(local, mesh=mesh, in_specs=in_specs, out_specs=out_specs, check_vma=False)
```

```python
import jax
import jax.numpy as jnp
from jax import lax
from jax.sharding import Mesh, PartitionSpec as P

EXPERTS = 32
PARAMS = 5261312


BETA_ONE = 0.9
BETA_TWO = 0.999
EPSILON = 1e-08
DECAY = 0.1

DP_PARTS = ("dp_x", "dp_z", "dp_core")
DP = DP_PARTS


def adam_update(grad_sum, master, first, second, clip, rate, first_fix, second_fix, mask):
    grad = clip * grad_sum
    momentum = BETA_ONE * first + (1.0 - BETA_ONE) * grad
    variance = BETA_TWO * second + (1.0 - BETA_TWO) * grad * grad
    update = (
        momentum / first_fix / (jnp.sqrt(variance / second_fix) + EPSILON) + DECAY * mask * master
    )
    renewed = master - rate * update
    return (renewed, momentum, variance, renewed.astype(jnp.bfloat16))


def local(
    attention_grads,
    expert_grads,
    routing_grads,
    attention_master,
    attention_first,
    attention_second,
    expert_master,
    expert_first,
    expert_second,
    routing_master,
    routing_first,
    routing_second,
    step_count,
    learn_rate,
    clip_level,
):
    n_dp = lax.axis_size(DP)
    n_t = lax.axis_size("tensor")
    t_idx = lax.axis_index("tensor")

    att = attention_grads[0, 0]
    exp = expert_grads[0, 0]
    rte = routing_grads[0, 0, 0]
    rows, cols = att.shape
    n_e, e_rows, e_cols = exp.shape
    n_r, r_cols = rte.shape
    ra = rows // n_dp
    re = e_rows // n_dp
    rc = r_cols // n_dp
    own = rc // n_t

    exp_rows = exp.transpose(1, 0, 2).reshape(e_rows, n_e * e_cols)
    send = jnp.concatenate([att, exp_rows, rte.T], axis=1)
    got = lax.all_to_all(send, DP, 0, 0, tiled=True)
    total = jnp.sum(got.reshape(n_dp, ra, -1).astype(jnp.float32), axis=0)
    attention_sum = total[:, :cols]
    expert_sum = total[:, cols : cols + n_e * e_cols].reshape(re, n_e, e_cols).transpose(1, 0, 2)
    route_part = total[:, cols + n_e * e_cols :].T

    local_squares = jnp.sum(attention_sum * attention_sum) + jnp.sum(expert_sum * expert_sum)
    slot = (jnp.arange(rc) // own == t_idx)[None, :]

    def placed(values):
        return jnp.where(slot, jnp.tile(values, (1, n_t)), 0.0)

    packed = jnp.stack(
        [
            route_part,
            placed(routing_master),
            placed(routing_first),
            placed(routing_second),
            jnp.full((n_r, rc), 0.0).at[0, 0].set(local_squares),
        ]
    )
    packed = lax.psum(packed, "tensor")
    route_sum = packed[0]
    route_master_blk, route_first_blk, route_second_blk = packed[1], packed[2], packed[3]
    group_squares = packed[4, 0, 0] + jnp.sum(route_sum * route_sum)

    spread = jnp.broadcast_to(group_squares, (n_dp, 1))
    squares = jnp.sum(lax.all_to_all(spread, DP, 0, 0, tiled=True))

    grad_norm = jnp.sqrt(squares)
    clip = jnp.minimum(1.0, clip_level[0] * jnp.sqrt(jnp.float32(PARAMS)) / (grad_norm + 1e-06))
    steps_done = step_count[0].astype(jnp.float32)
    first_fix = 1.0 - jnp.power(jnp.float32(BETA_ONE), steps_done)
    second_fix = 1.0 - jnp.power(jnp.float32(BETA_TWO), steps_done)
    rate = learn_rate[0]
    one = jnp.float32(1.0)
    attention_out = adam_update(
        attention_sum, attention_master, attention_first, attention_second,
        clip, rate, first_fix, second_fix, one,
    )
    expert_out = adam_update(
        expert_sum, expert_master, expert_first, expert_second,
        clip, rate, first_fix, second_fix, one,
    )
    row_index = jnp.arange(n_r, dtype=jnp.int32)
    routing_mask = (row_index < EXPERTS).astype(jnp.float32)[:, None]
    routing_out = adam_update(
        route_sum, route_master_blk, route_first_blk, route_second_blk,
        clip, rate, first_fix, second_fix, routing_mask,
    )

    def mine(values):
        return lax.dynamic_slice_in_dim(values, t_idx * own, own, axis=1)

    def gather(values):
        sizes = [lax.axis_size(name) for name in DP_PARTS]
        for name in (DP_PARTS[1], DP_PARTS[0], DP_PARTS[2]):
            values = lax.all_gather(values, name, axis=0, tiled=True)
        blocks = values.reshape(sizes[2], sizes[0], sizes[1], -1, values.shape[-1])
        return blocks.transpose(1, 2, 0, 3, 4).reshape(values.shape)

    rest = jnp.concatenate(
        [
            attention_out[3],
            expert_out[3].transpose(1, 0, 2).reshape(re, n_e * e_cols),
            routing_out[3].T,
        ],
        axis=1,
    )
    rest = gather(rest)
    attention_served = rest[:, :cols]
    expert_served = (
        rest[:, cols : cols + n_e * e_cols].reshape(e_rows, n_e, e_cols).transpose(1, 0, 2)
    )
    routing_served = rest[:, cols + n_e * e_cols :].T
    return (
        attention_out[0],
        attention_out[1],
        attention_out[2],
        attention_served,
        expert_out[0],
        expert_out[1],
        expert_out[2],
        expert_served,
        mine(routing_out[0]),
        mine(routing_out[1]),
        mine(routing_out[2]),
        routing_served,
    )


def split_mesh(mesh):
    column = mesh.devices[:, 0]
    sizes = (
        len({d.coords[0] for d in column}),
        len({d.coords[2] for d in column}),
        len({d.core_on_chip for d in column}),
    )
    devices = mesh.devices.reshape(sizes + mesh.devices.shape[1:])
    return Mesh(devices, DP_PARTS + ("tensor",))


def solution(mesh):
    mesh = split_mesh(mesh)
    in_specs = (
        P(DP, None, None, "tensor"),
        P(DP, None, None, None, "tensor"),
        P(DP, "tensor", None, None, None),
        P(DP, "tensor"),
        P(DP, "tensor"),
        P(DP, "tensor"),
        P(None, DP, "tensor"),
        P(None, DP, "tensor"),
        P(None, DP, "tensor"),
        P(None, (DP + ("tensor",))),
        P(None, (DP + ("tensor",))),
        P(None, (DP + ("tensor",))),
        P(),
        P(),
        P(),
    )
    out_specs = (
        P(DP, "tensor"),
        P(DP, "tensor"),
        P(DP, "tensor"),
        P(None, "tensor"),
        P(None, DP, "tensor"),
        P(None, DP, "tensor"),
        P(None, DP, "tensor"),
        P(None, None, "tensor"),
        P(None, (DP + ("tensor",))),
        P(None, (DP + ("tensor",))),
        P(None, (DP + ("tensor",))),
        P(),
    )
    return jax.shard_map(local, mesh=mesh, in_specs=in_specs, out_specs=out_specs, check_vma=False)
```

```python
import jax
import jax.numpy as jnp
from jax import lax
from jax.sharding import Mesh, PartitionSpec as P

EXPERTS = 32
PARAMS = 5261312


BETA_ONE = 0.9
BETA_TWO = 0.999
EPSILON = 1e-08
DECAY = 0.1

DP_PARTS = ("dp_x", "dp_z", "dp_core")
DP = DP_PARTS


def adam_update(grad_sum, master, first, second, clip, rate, first_fix, second_fix, mask):
    grad = clip * grad_sum
    momentum = BETA_ONE * first + (1.0 - BETA_ONE) * grad
    variance = BETA_TWO * second + (1.0 - BETA_TWO) * grad * grad
    update = (
        momentum / first_fix / (jnp.sqrt(variance / second_fix) + EPSILON) + DECAY * mask * master
    )
    renewed = master - rate * update
    return (renewed, momentum, variance, renewed.astype(jnp.bfloat16))


def local(
    attention_grads,
    expert_grads,
    routing_grads,
    attention_master,
    attention_first,
    attention_second,
    expert_master,
    expert_first,
    expert_second,
    routing_master,
    routing_first,
    routing_second,
    step_count,
    learn_rate,
    clip_level,
):
    n_dp = lax.axis_size(DP)
    n_t = lax.axis_size("tensor")
    t_idx = lax.axis_index("tensor")

    att = attention_grads[0, 0]
    exp = expert_grads[0, 0]
    rte = routing_grads[0, 0, 0]
    rows, cols = att.shape
    n_e, e_rows, e_cols = exp.shape
    n_r, r_cols = rte.shape
    ra = rows // n_dp
    re = e_rows // n_dp
    rc = r_cols // n_dp
    own = rc // n_t

    exp_rows = exp.transpose(1, 0, 2).reshape(e_rows, n_e * e_cols)
    send = jnp.concatenate([att, exp_rows, rte.T], axis=1)
    got = lax.all_to_all(send, DP, 0, 0, tiled=True)
    total = jnp.sum(got.reshape(n_dp, ra, -1).astype(jnp.float32), axis=0)
    attention_sum = total[:, :cols]
    expert_sum = total[:, cols : cols + n_e * e_cols].reshape(re, n_e, e_cols).transpose(1, 0, 2)
    route_part = total[:, cols + n_e * e_cols :].T

    local_squares = jnp.sum(attention_sum * attention_sum) + jnp.sum(expert_sum * expert_sum)
    slot = (jnp.arange(rc) // own == t_idx)[None, :]

    def placed(values):
        return jnp.where(slot, jnp.tile(values, (1, n_t)), 0.0)

    packed = jnp.stack(
        [
            route_part,
            placed(routing_master),
            placed(routing_first),
            placed(routing_second),
            jnp.full((n_r, rc), 0.0).at[0, 0].set(local_squares),
        ]
    )
    packed = lax.psum(packed, "tensor")
    route_sum = packed[0]
    route_master_blk, route_first_blk, route_second_blk = packed[1], packed[2], packed[3]
    group_squares = packed[4, 0, 0] + jnp.sum(route_sum * route_sum)

    spread = jnp.broadcast_to(group_squares, (n_dp, 1))
    squares = jnp.sum(lax.all_to_all(spread, DP, 0, 0, tiled=True))

    grad_norm = jnp.sqrt(squares)
    clip = jnp.minimum(1.0, clip_level[0] * jnp.sqrt(jnp.float32(PARAMS)) / (grad_norm + 1e-06))
    steps_done = step_count[0].astype(jnp.float32)
    first_fix = 1.0 - jnp.power(jnp.float32(BETA_ONE), steps_done)
    second_fix = 1.0 - jnp.power(jnp.float32(BETA_TWO), steps_done)
    rate = learn_rate[0]
    one = jnp.float32(1.0)
    attention_out = adam_update(
        attention_sum, attention_master, attention_first, attention_second,
        clip, rate, first_fix, second_fix, one,
    )
    expert_out = adam_update(
        expert_sum, expert_master, expert_first, expert_second,
        clip, rate, first_fix, second_fix, one,
    )
    row_index = jnp.arange(n_r, dtype=jnp.int32)
    routing_mask = (row_index < EXPERTS).astype(jnp.float32)[:, None]
    routing_out = adam_update(
        route_sum, route_master_blk, route_first_blk, route_second_blk,
        clip, rate, first_fix, second_fix, routing_mask,
    )

    def mine(values):
        return lax.dynamic_slice_in_dim(values, t_idx * own, own, axis=1)

    def gather(values):
        for name in (DP_PARTS[2], DP_PARTS[1]):
            values = lax.all_gather(values, name, axis=0, tiled=True)
        name = DP_PARTS[0]
        size = lax.axis_size(name)
        ring = [values] + [
            lax.ppermute(values, name, [(i, (i + size - k) % size) for i in range(size)])
            for k in range(1, size)
        ]
        stacked = jnp.stack(ring)
        stacked = jnp.roll(stacked, lax.axis_index(name), axis=0)
        return stacked.reshape((-1,) + values.shape[1:])

    rest = jnp.concatenate(
        [
            attention_out[3],
            expert_out[3].transpose(1, 0, 2).reshape(re, n_e * e_cols),
            routing_out[3].T,
        ],
        axis=1,
    )
    rest = gather(rest)
    attention_served = rest[:, :cols]
    expert_served = (
        rest[:, cols : cols + n_e * e_cols].reshape(e_rows, n_e, e_cols).transpose(1, 0, 2)
    )
    routing_served = rest[:, cols + n_e * e_cols :].T
    return (
        attention_out[0],
        attention_out[1],
        attention_out[2],
        attention_served,
        expert_out[0],
        expert_out[1],
        expert_out[2],
        expert_served,
        mine(routing_out[0]),
        mine(routing_out[1]),
        mine(routing_out[2]),
        routing_served,
    )


def split_mesh(mesh):
    column = mesh.devices[:, 0]
    sizes = (
        len({d.coords[0] for d in column}),
        len({d.coords[2] for d in column}),
        len({d.core_on_chip for d in column}),
    )
    devices = mesh.devices.reshape(sizes + mesh.devices.shape[1:])
    return Mesh(devices, DP_PARTS + ("tensor",))


def solution(mesh):
    mesh = split_mesh(mesh)
    in_specs = (
        P(DP, None, None, "tensor"),
        P(DP, None, None, None, "tensor"),
        P(DP, "tensor", None, None, None),
        P(DP, "tensor"),
        P(DP, "tensor"),
        P(DP, "tensor"),
        P(None, DP, "tensor"),
        P(None, DP, "tensor"),
        P(None, DP, "tensor"),
        P(None, (DP + ("tensor",))),
        P(None, (DP + ("tensor",))),
        P(None, (DP + ("tensor",))),
        P(),
        P(),
        P(),
    )
    out_specs = (
        P(DP, "tensor"),
        P(DP, "tensor"),
        P(DP, "tensor"),
        P(None, "tensor"),
        P(None, DP, "tensor"),
        P(None, DP, "tensor"),
        P(None, DP, "tensor"),
        P(None, None, "tensor"),
        P(None, (DP + ("tensor",))),
        P(None, (DP + ("tensor",))),
        P(None, (DP + ("tensor",))),
        P(),
    )
    return jax.shard_map(local, mesh=mesh, in_specs=in_specs, out_specs=out_specs, check_vma=False)
```

```python
import jax
import jax.numpy as jnp
from jax import lax
from jax.sharding import Mesh, PartitionSpec as P

EXPERTS = 32

PARAMS = 5261312


BETA_ONE = 0.9
BETA_TWO = 0.999
EPSILON = 1e-08
DECAY = 0.1

DP_PARTS = ("dp_x", "dp_z", "dp_core")
DP = DP_PARTS


def adam_update(grad_sum, master, first, second, clip, rate, first_fix, second_fix, mask):
    grad = clip * grad_sum
    momentum = BETA_ONE * first + (1.0 - BETA_ONE) * grad
    variance = BETA_TWO * second + (1.0 - BETA_TWO) * grad * grad
    update = (
        momentum / first_fix / (jnp.sqrt(variance / second_fix) + EPSILON) + DECAY * mask * master
    )
    renewed = master - rate * update
    return (renewed, momentum, variance, renewed.astype(jnp.bfloat16))


def local(
    attention_grads,
    expert_grads,
    routing_grads,
    attention_master,
    attention_first,
    attention_second,
    expert_master,
    expert_first,
    expert_second,
    routing_master,
    routing_first,
    routing_second,
    step_count,
    learn_rate,
    clip_level,
):
    n_dp = lax.axis_size(DP)
    n_t = lax.axis_size("tensor")
    t_idx = lax.axis_index("tensor")

    att = attention_grads[0, 0]
    exp = expert_grads[0, 0]
    rte = routing_grads[0, 0, 0]
    rows, cols = att.shape
    n_e, e_rows, e_cols = exp.shape
    n_r, r_cols = rte.shape
    ra = rows // n_dp
    re = e_rows // n_dp
    rc = r_cols // n_dp
    own = rc // n_t

    exp_rows = exp.transpose(1, 0, 2).reshape(e_rows, n_e * e_cols)
    send = jnp.concatenate([att, exp_rows, rte.T], axis=1)
    got = lax.all_to_all(send, DP, 0, 0, tiled=True)
    total = jnp.sum(got.reshape(n_dp, ra, -1).astype(jnp.float32), axis=0)
    attention_sum = total[:, :cols]
    expert_sum = total[:, cols : cols + n_e * e_cols].reshape(re, n_e, e_cols).transpose(1, 0, 2)
    route_part = total[:, cols + n_e * e_cols :].T

    local_squares = jnp.sum(attention_sum * attention_sum) + jnp.sum(expert_sum * expert_sum)
    slot = (jnp.arange(rc) // own == t_idx)[None, :]

    def placed(values):
        return jnp.where(slot, jnp.tile(values, (1, n_t)), 0.0)

    packed = jnp.stack(
        [
            route_part,
            placed(routing_master),
            placed(routing_first),
            placed(routing_second),
            jnp.full((n_r, rc), 0.0).at[0, 0].set(local_squares),
        ]
    )
    packed = lax.psum(packed, "tensor")
    route_sum = packed[0]
    route_master_blk, route_first_blk, route_second_blk = packed[1], packed[2], packed[3]
    group_squares = packed[4, 0, 0] + jnp.sum(route_sum * route_sum)

    spread = jnp.broadcast_to(group_squares, (n_dp, 1))
    squares = jnp.sum(lax.all_to_all(spread, DP, 0, 0, tiled=True))

    grad_norm = jnp.sqrt(squares)
    clip = jnp.minimum(1.0, clip_level[0] * jnp.sqrt(jnp.float32(PARAMS)) / (grad_norm + 1e-06))
    steps_done = step_count[0].astype(jnp.float32)
    first_fix = 1.0 - jnp.power(jnp.float32(BETA_ONE), steps_done)
    second_fix = 1.0 - jnp.power(jnp.float32(BETA_TWO), steps_done)
    rate = learn_rate[0]
    one = jnp.float32(1.0)
    attention_out = adam_update(
        attention_sum, attention_master, attention_first, attention_second,
        clip, rate, first_fix, second_fix, one,
    )
    expert_out = adam_update(
        expert_sum, expert_master, expert_first, expert_second,
        clip, rate, first_fix, second_fix, one,
    )
    row_index = jnp.arange(n_r, dtype=jnp.int32)
    routing_mask = (row_index < EXPERTS).astype(jnp.float32)[:, None]
    routing_out = adam_update(
        route_sum, route_master_blk, route_first_blk, route_second_blk,
        clip, rate, first_fix, second_fix, routing_mask,
    )

    def mine(values):
        return lax.dynamic_slice_in_dim(values, t_idx * own, own, axis=1)

    def ring_gather(values, name):
        size = lax.axis_size(name)
        ring = [values] + [
            lax.ppermute(values, name, [(i, (i + size - k) % size) for i in range(size)])
            for k in range(1, size)
        ]
        stacked = jnp.stack(ring)
        stacked = jnp.roll(stacked, lax.axis_index(name), axis=0)
        return stacked.reshape((-1,) + values.shape[1:])

    def gather(values):
        values = lax.all_gather(values, DP_PARTS[2], axis=0, tiled=True)
        values = ring_gather(values, DP_PARTS[1])
        return ring_gather(values, DP_PARTS[0])

    rest = jnp.concatenate(
        [
            attention_out[3],
            expert_out[3].transpose(1, 0, 2).reshape(re, n_e * e_cols),
            routing_out[3].T,
        ],
        axis=1,
    )
    rest = gather(rest)
    attention_served = rest[:, :cols]
    expert_served = (
        rest[:, cols : cols + n_e * e_cols].reshape(e_rows, n_e, e_cols).transpose(1, 0, 2)
    )
    routing_served = rest[:, cols + n_e * e_cols :].T
    return (
        attention_out[0],
        attention_out[1],
        attention_out[2],
        attention_served,
        expert_out[0],
        expert_out[1],
        expert_out[2],
        expert_served,
        mine(routing_out[0]),
        mine(routing_out[1]),
        mine(routing_out[2]),
        routing_served,
    )


def split_mesh(mesh):
    column = mesh.devices[:, 0]
    sizes = (
        len({d.coords[0] for d in column}),
        len({d.coords[2] for d in column}),
        len({d.core_on_chip for d in column}),
    )
    devices = mesh.devices.reshape(sizes + mesh.devices.shape[1:])
    return Mesh(devices, DP_PARTS + ("tensor",))


def solution(mesh):
    mesh = split_mesh(mesh)
    in_specs = (
        P(DP, None, None, "tensor"),
        P(DP, None, None, None, "tensor"),
        P(DP, "tensor", None, None, None),
        P(DP, "tensor"),
        P(DP, "tensor"),
        P(DP, "tensor"),
        P(None, DP, "tensor"),
        P(None, DP, "tensor"),
        P(None, DP, "tensor"),
        P(None, (DP + ("tensor",))),
        P(None, (DP + ("tensor",))),
        P(None, (DP + ("tensor",))),
        P(),
        P(),
        P(),
    )
    out_specs = (
        P(DP, "tensor"),
        P(DP, "tensor"),
        P(DP, "tensor"),
        P(None, "tensor"),
        P(None, DP, "tensor"),
        P(None, DP, "tensor"),
        P(None, DP, "tensor"),
        P(None, None, "tensor"),
        P(None, (DP + ("tensor",))),
        P(None, (DP + ("tensor",))),
        P(None, (DP + ("tensor",))),
        P(),
    )
    return jax.shard_map(local, mesh=mesh, in_specs=in_specs, out_specs=out_specs, check_vma=False)
```

```python
import jax
import jax.numpy as jnp
from jax import lax
from jax.sharding import Mesh, PartitionSpec as P

EXPERTS = 32

PARAMS = 5261312


BETA_ONE = 0.9
BETA_TWO = 0.999
EPSILON = 1e-08
DECAY = 0.1

DP_PARTS = ("dp_x", "dp_z", "dp_core")
DP = DP_PARTS


def adam_update(grad_sum, master, first, second, clip, rate, first_fix, second_fix, mask):
    grad = clip * grad_sum
    momentum = BETA_ONE * first + (1.0 - BETA_ONE) * grad
    variance = BETA_TWO * second + (1.0 - BETA_TWO) * grad * grad
    update = (
        momentum / first_fix / (jnp.sqrt(variance / second_fix) + EPSILON) + DECAY * mask * master
    )
    renewed = master - rate * update
    return (renewed, momentum, variance, renewed.astype(jnp.bfloat16))


def local(
    attention_grads,
    expert_grads,
    routing_grads,
    attention_master,
    attention_first,
    attention_second,
    expert_master,
    expert_first,
    expert_second,
    routing_master,
    routing_first,
    routing_second,
    step_count,
    learn_rate,
    clip_level,
):
    n_dp = lax.axis_size(DP)
    n_t = lax.axis_size("tensor")
    t_idx = lax.axis_index("tensor")

    att = attention_grads[0, 0]
    exp = expert_grads[0, 0]
    rte = routing_grads[0, 0, 0]
    rows, cols = att.shape
    n_e, e_rows, e_cols = exp.shape
    n_r, r_cols = rte.shape
    ra = rows // n_dp
    re = e_rows // n_dp
    rc = r_cols // n_dp
    own = rc // n_t

    exp_rows = exp.transpose(1, 0, 2).reshape(e_rows, n_e * e_cols)
    send = jnp.concatenate([att, exp_rows, rte.T], axis=1)
    got = lax.all_to_all(send, DP, 0, 0, tiled=True)
    total = jnp.sum(got.reshape(n_dp, ra, -1).astype(jnp.float32), axis=0)
    attention_sum = total[:, :cols]
    expert_sum = total[:, cols : cols + n_e * e_cols].reshape(re, n_e, e_cols).transpose(1, 0, 2)
    route_part = total[:, cols + n_e * e_cols :].T

    local_squares = jnp.sum(attention_sum * attention_sum) + jnp.sum(expert_sum * expert_sum)
    slot = (jnp.arange(rc) // own == t_idx)[None, :]

    def placed(values):
        return jnp.where(slot, jnp.tile(values, (1, n_t)), 0.0)

    packed = jnp.stack(
        [
            route_part,
            placed(routing_master),
            placed(routing_first),
            placed(routing_second),
            jnp.full((n_r, rc), 0.0).at[0, 0].set(local_squares),
        ]
    )
    packed = lax.psum(packed, "tensor")
    route_sum = packed[0]
    route_master_blk, route_first_blk, route_second_blk = packed[1], packed[2], packed[3]
    group_squares = packed[4, 0, 0] + jnp.sum(route_sum * route_sum)

    spread = jnp.broadcast_to(group_squares, (n_dp, 1))
    squares = jnp.sum(lax.all_to_all(spread, DP, 0, 0, tiled=True))

    grad_norm = jnp.sqrt(squares)
    clip = jnp.minimum(1.0, clip_level[0] * jnp.sqrt(jnp.float32(PARAMS)) / (grad_norm + 1e-06))
    steps_done = step_count[0].astype(jnp.float32)
    first_fix = 1.0 - jnp.power(jnp.float32(BETA_ONE), steps_done)
    second_fix = 1.0 - jnp.power(jnp.float32(BETA_TWO), steps_done)
    rate = learn_rate[0]
    one = jnp.float32(1.0)
    attention_out = adam_update(
        attention_sum, attention_master, attention_first, attention_second,
        clip, rate, first_fix, second_fix, one,
    )
    expert_out = adam_update(
        expert_sum, expert_master, expert_first, expert_second,
        clip, rate, first_fix, second_fix, one,
    )
    row_index = jnp.arange(n_r, dtype=jnp.int32)
    routing_mask = (row_index < EXPERTS).astype(jnp.float32)[:, None]
    routing_out = adam_update(
        route_sum, route_master_blk, route_first_blk, route_second_blk,
        clip, rate, first_fix, second_fix, routing_mask,
    )

    def mine(values):
        return lax.dynamic_slice_in_dim(values, t_idx * own, own, axis=1)

    def ring_gather(values, name):
        size = lax.axis_size(name)
        ring = [values] + [
            lax.ppermute(values, name, [(i, (i + size - k) % size) for i in range(size)])
            for k in range(1, size)
        ]
        stacked = jnp.stack(ring)
        stacked = jnp.roll(stacked, lax.axis_index(name), axis=0)
        return stacked.reshape((-1,) + values.shape[1:])

    def gather(values):
        sizes = [lax.axis_size(name) for name in DP_PARTS]
        for name in (DP_PARTS[1], DP_PARTS[0], DP_PARTS[2]):
            values = ring_gather(values, name)
        blocks = values.reshape(sizes[2], sizes[0], sizes[1], -1, values.shape[-1])
        return blocks.transpose(1, 2, 0, 3, 4).reshape(values.shape)

    rest = jnp.concatenate(
        [
            attention_out[3],
            expert_out[3].transpose(1, 0, 2).reshape(re, n_e * e_cols),
            routing_out[3].T,
        ],
        axis=1,
    )
    rest = gather(rest)
    attention_served = rest[:, :cols]
    expert_served = (
        rest[:, cols : cols + n_e * e_cols].reshape(e_rows, n_e, e_cols).transpose(1, 0, 2)
    )
    routing_served = rest[:, cols + n_e * e_cols :].T
    return (
        attention_out[0],
        attention_out[1],
        attention_out[2],
        attention_served,
        expert_out[0],
        expert_out[1],
        expert_out[2],
        expert_served,
        mine(routing_out[0]),
        mine(routing_out[1]),
        mine(routing_out[2]),
        routing_served,
    )


def split_mesh(mesh):
    column = mesh.devices[:, 0]
    sizes = (
        len({d.coords[0] for d in column}),
        len({d.coords[2] for d in column}),
        len({d.core_on_chip for d in column}),
    )
    devices = mesh.devices.reshape(sizes + mesh.devices.shape[1:])
    return Mesh(devices, DP_PARTS + ("tensor",))


def solution(mesh):
    mesh = split_mesh(mesh)
    in_specs = (
        P(DP, None, None, "tensor"),
        P(DP, None, None, None, "tensor"),
        P(DP, "tensor", None, None, None),
        P(DP, "tensor"),
        P(DP, "tensor"),
        P(DP, "tensor"),
        P(None, DP, "tensor"),
        P(None, DP, "tensor"),
        P(None, DP, "tensor"),
        P(None, (DP + ("tensor",))),
        P(None, (DP + ("tensor",))),
        P(None, (DP + ("tensor",))),
        P(),
        P(),
        P(),
    )
    out_specs = (
        P(DP, "tensor"),
        P(DP, "tensor"),
        P(DP, "tensor"),
        P(None, "tensor"),
        P(None, DP, "tensor"),
        P(None, DP, "tensor"),
        P(None, DP, "tensor"),
        P(None, None, "tensor"),
        P(None, (DP + ("tensor",))),
        P(None, (DP + ("tensor",))),
        P(None, (DP + ("tensor",))),
        P(),
    )
    return jax.shard_map(local, mesh=mesh, in_specs=in_specs, out_specs=out_specs, check_vma=False)
```

```python
import jax
import jax.numpy as jnp
from jax import lax
from jax.sharding import Mesh, PartitionSpec as P

EXPERTS = 32

PARAMS = 5261312


BETA_ONE = 0.9
BETA_TWO = 0.999
EPSILON = 1e-08
DECAY = 0.1

DP_PARTS = ("dp_x", "dp_z", "dp_core")
DP = DP_PARTS


def adam_update(grad_sum, master, first, second, clip, rate, first_fix, second_fix, mask):
    grad = clip * grad_sum
    momentum = BETA_ONE * first + (1.0 - BETA_ONE) * grad
    variance = BETA_TWO * second + (1.0 - BETA_TWO) * grad * grad
    update = (
        momentum / first_fix / (jnp.sqrt(variance / second_fix) + EPSILON) + DECAY * mask * master
    )
    renewed = master - rate * update
    return (renewed, momentum, variance, renewed.astype(jnp.bfloat16))


def reduce_scatter(blocks):
    for position, name in ((1, DP_PARTS[1]), (0, DP_PARTS[0]), (0, DP_PARTS[2])):
        size = lax.axis_size(name)
        index = lax.axis_index(name)
        total = jnp.take(blocks, index, axis=position).astype(jnp.float32)
        for k in range(1, size):
            piece = jnp.take(blocks, (index + k) % size, axis=position)
            got = lax.ppermute(piece, name, [(i, (i + k) % size) for i in range(size)])
            total = total + got.astype(jnp.float32)
        blocks = total
    return blocks


def local(
    attention_grads,
    expert_grads,
    routing_grads,
    attention_master,
    attention_first,
    attention_second,
    expert_master,
    expert_first,
    expert_second,
    routing_master,
    routing_first,
    routing_second,
    step_count,
    learn_rate,
    clip_level,
):
    n_dp = lax.axis_size(DP)
    n_t = lax.axis_size("tensor")
    t_idx = lax.axis_index("tensor")

    att = attention_grads[0, 0]
    exp = expert_grads[0, 0]
    rte = routing_grads[0, 0, 0]
    rows, cols = att.shape
    n_e, e_rows, e_cols = exp.shape
    n_r, r_cols = rte.shape
    ra = rows // n_dp
    re = e_rows // n_dp
    rc = r_cols // n_dp
    own = rc // n_t

    exp_rows = exp.transpose(1, 0, 2).reshape(e_rows, n_e * e_cols)
    send = jnp.concatenate([att, exp_rows, rte.T], axis=1)
    sizes = [lax.axis_size(name) for name in DP_PARTS]
    total = reduce_scatter(send.reshape(tuple(sizes) + (ra, -1)))

    attention_sum = total[:, :cols]
    expert_sum = total[:, cols : cols + n_e * e_cols].reshape(re, n_e, e_cols).transpose(1, 0, 2)
    route_part = total[:, cols + n_e * e_cols :].T

    local_squares = jnp.sum(attention_sum * attention_sum) + jnp.sum(expert_sum * expert_sum)
    slot = (jnp.arange(rc) // own == t_idx)[None, :]

    def placed(values):
        return jnp.where(slot, jnp.tile(values, (1, n_t)), 0.0)

    packed = jnp.stack(
        [
            route_part,
            placed(routing_master),
            placed(routing_first),
            placed(routing_second),
            jnp.full((n_r, rc), 0.0).at[0, 0].set(local_squares),
        ]
    )
    packed = lax.psum(packed, "tensor")
    route_sum = packed[0]
    route_master_blk, route_first_blk, route_second_blk = packed[1], packed[2], packed[3]
    group_squares = packed[4, 0, 0] + jnp.sum(route_sum * route_sum)

    spread = jnp.broadcast_to(group_squares, (n_dp, 1))
    squares = jnp.sum(lax.all_to_all(spread, DP, 0, 0, tiled=True))

    grad_norm = jnp.sqrt(squares)
    clip = jnp.minimum(1.0, clip_level[0] * jnp.sqrt(jnp.float32(PARAMS)) / (grad_norm + 1e-06))
    steps_done = step_count[0].astype(jnp.float32)
    first_fix = 1.0 - jnp.power(jnp.float32(BETA_ONE), steps_done)
    second_fix = 1.0 - jnp.power(jnp.float32(BETA_TWO), steps_done)
    rate = learn_rate[0]
    one = jnp.float32(1.0)
    attention_out = adam_update(
        attention_sum, attention_master, attention_first, attention_second,
        clip, rate, first_fix, second_fix, one,
    )
    expert_out = adam_update(
        expert_sum, expert_master, expert_first, expert_second,
        clip, rate, first_fix, second_fix, one,
    )
    row_index = jnp.arange(n_r, dtype=jnp.int32)
    routing_mask = (row_index < EXPERTS).astype(jnp.float32)[:, None]
    routing_out = adam_update(
        route_sum, route_master_blk, route_first_blk, route_second_blk,
        clip, rate, first_fix, second_fix, routing_mask,
    )

    def mine(values):
        return lax.dynamic_slice_in_dim(values, t_idx * own, own, axis=1)

    def ring_gather(values, name):
        size = lax.axis_size(name)
        ring = [values] + [
            lax.ppermute(values, name, [(i, (i + size - k) % size) for i in range(size)])
            for k in range(1, size)
        ]
        stacked = jnp.stack(ring)
        stacked = jnp.roll(stacked, lax.axis_index(name), axis=0)
        return stacked.reshape((-1,) + values.shape[1:])

    def gather(values):
        sizes = [lax.axis_size(name) for name in DP_PARTS]
        for name in (DP_PARTS[1], DP_PARTS[0], DP_PARTS[2]):
            values = ring_gather(values, name)
        blocks = values.reshape(sizes[2], sizes[0], sizes[1], -1, values.shape[-1])
        return blocks.transpose(1, 2, 0, 3, 4).reshape(values.shape)

    rest = jnp.concatenate(
        [
            attention_out[3],
            expert_out[3].transpose(1, 0, 2).reshape(re, n_e * e_cols),
            routing_out[3].T,
        ],
        axis=1,
    )
    rest = gather(rest)
    attention_served = rest[:, :cols]
    expert_served = (
        rest[:, cols : cols + n_e * e_cols].reshape(e_rows, n_e, e_cols).transpose(1, 0, 2)
    )
    routing_served = rest[:, cols + n_e * e_cols :].T
    return (
        attention_out[0],
        attention_out[1],
        attention_out[2],
        attention_served,
        expert_out[0],
        expert_out[1],
        expert_out[2],
        expert_served,
        mine(routing_out[0]),
        mine(routing_out[1]),
        mine(routing_out[2]),
        routing_served,
    )


def split_mesh(mesh):
    column = mesh.devices[:, 0]
    sizes = (
        len({d.coords[0] for d in column}),
        len({d.coords[2] for d in column}),
        len({d.core_on_chip for d in column}),
    )
    devices = mesh.devices.reshape(sizes + mesh.devices.shape[1:])
    return Mesh(devices, DP_PARTS + ("tensor",))


def solution(mesh):
    mesh = split_mesh(mesh)
    in_specs = (
        P(DP, None, None, "tensor"),
        P(DP, None, None, None, "tensor"),
        P(DP, "tensor", None, None, None),
        P(DP, "tensor"),
        P(DP, "tensor"),
        P(DP, "tensor"),
        P(None, DP, "tensor"),
        P(None, DP, "tensor"),
        P(None, DP, "tensor"),
        P(None, (DP + ("tensor",))),
        P(None, (DP + ("tensor",))),
        P(None, (DP + ("tensor",))),
        P(),
        P(),
        P(),
    )
    out_specs = (
        P(DP, "tensor"),
        P(DP, "tensor"),
        P(DP, "tensor"),
        P(None, "tensor"),
        P(None, DP, "tensor"),
        P(None, DP, "tensor"),
        P(None, DP, "tensor"),
        P(None, None, "tensor"),
        P(None, (DP + ("tensor",))),
        P(None, (DP + ("tensor",))),
        P(None, (DP + ("tensor",))),
        P(),
    )
    return jax.shard_map(local, mesh=mesh, in_specs=in_specs, out_specs=out_specs, check_vma=False)
```

```python
import jax
import jax.numpy as jnp
from jax import lax
from jax.sharding import Mesh, PartitionSpec as P

EXPERTS = 32

PARAMS = 5261312


BETA_ONE = 0.9
BETA_TWO = 0.999
EPSILON = 1e-08
DECAY = 0.1

DP_PARTS = ("dp_x", "dp_z", "dp_core")
DP = DP_PARTS


def adam_update(grad_sum, master, first, second, clip, rate, first_fix, second_fix, mask):
    grad = clip * grad_sum
    momentum = BETA_ONE * first + (1.0 - BETA_ONE) * grad
    variance = BETA_TWO * second + (1.0 - BETA_TWO) * grad * grad
    update = (
        momentum / first_fix / (jnp.sqrt(variance / second_fix) + EPSILON) + DECAY * mask * master
    )
    renewed = master - rate * update
    return (renewed, momentum, variance, renewed.astype(jnp.bfloat16))


def local(
    attention_grads,
    expert_grads,
    routing_grads,
    attention_master,
    attention_first,
    attention_second,
    expert_master,
    expert_first,
    expert_second,
    routing_master,
    routing_first,
    routing_second,
    step_count,
    learn_rate,
    clip_level,
):
    n_dp = lax.axis_size(DP)
    n_t = lax.axis_size("tensor")
    t_idx = lax.axis_index("tensor")

    att = attention_grads[0, 0]
    exp = expert_grads[0, 0]
    rte = routing_grads[0, 0, 0]
    rows, cols = att.shape
    n_e, e_rows, e_cols = exp.shape
    n_r, r_cols = rte.shape
    ra = rows // n_dp
    re = e_rows // n_dp
    rc = r_cols // n_dp
    own = rc // n_t

    exp_rows = exp.transpose(1, 0, 2).reshape(e_rows, n_e * e_cols)
    send = jnp.concatenate([att, exp_rows, rte.T], axis=1)
    got = lax.all_to_all(send, DP, 0, 0, tiled=True)
    total = jnp.sum(got.reshape(n_dp, ra, -1).astype(jnp.float32), axis=0)
    attention_sum = total[:, :cols]
    expert_sum = total[:, cols : cols + n_e * e_cols].reshape(re, n_e, e_cols).transpose(1, 0, 2)
    route_part = total[:, cols + n_e * e_cols :].T

    local_squares = jnp.sum(attention_sum * attention_sum) + jnp.sum(expert_sum * expert_sum)
    slot = (jnp.arange(rc) // own == t_idx)[None, :]

    def placed(values):
        return jnp.where(slot, jnp.tile(values, (1, n_t)), 0.0)

    packed = jnp.stack(
        [
            route_part,
            placed(routing_master),
            placed(routing_first),
            placed(routing_second),
            jnp.full((n_r, rc), 0.0).at[0, 0].set(local_squares),
        ]
    )
    size = lax.axis_size("tensor")
    ring = [packed] + [
        lax.ppermute(packed, "tensor", [(i, (i + size - k) % size) for i in range(size)])
        for k in range(1, size)
    ]
    ring = jnp.roll(jnp.stack(ring), lax.axis_index("tensor"), axis=0)
    packed = jnp.sum(ring, axis=0)
    route_sum = packed[0]
    route_master_blk, route_first_blk, route_second_blk = packed[1], packed[2], packed[3]
    group_squares = packed[4, 0, 0] + jnp.sum(route_sum * route_sum)

    spread = jnp.broadcast_to(group_squares, (n_dp, 1))
    squares = jnp.sum(lax.all_to_all(spread, DP, 0, 0, tiled=True))

    grad_norm = jnp.sqrt(squares)
    clip = jnp.minimum(1.0, clip_level[0] * jnp.sqrt(jnp.float32(PARAMS)) / (grad_norm + 1e-06))
    steps_done = step_count[0].astype(jnp.float32)
    first_fix = 1.0 - jnp.power(jnp.float32(BETA_ONE), steps_done)
    second_fix = 1.0 - jnp.power(jnp.float32(BETA_TWO), steps_done)
    rate = learn_rate[0]
    one = jnp.float32(1.0)
    attention_out = adam_update(
        attention_sum, attention_master, attention_first, attention_second,
        clip, rate, first_fix, second_fix, one,
    )
    expert_out = adam_update(
        expert_sum, expert_master, expert_first, expert_second,
        clip, rate, first_fix, second_fix, one,
    )
    row_index = jnp.arange(n_r, dtype=jnp.int32)
    routing_mask = (row_index < EXPERTS).astype(jnp.float32)[:, None]
    routing_out = adam_update(
        route_sum, route_master_blk, route_first_blk, route_second_blk,
        clip, rate, first_fix, second_fix, routing_mask,
    )

    def mine(values):
        return lax.dynamic_slice_in_dim(values, t_idx * own, own, axis=1)

    def ring_gather(values, name):
        size = lax.axis_size(name)
        ring = [values] + [
            lax.ppermute(values, name, [(i, (i + size - k) % size) for i in range(size)])
            for k in range(1, size)
        ]
        stacked = jnp.stack(ring)
        stacked = jnp.roll(stacked, lax.axis_index(name), axis=0)
        return stacked.reshape((-1,) + values.shape[1:])

    def gather(values):
        sizes = [lax.axis_size(name) for name in DP_PARTS]
        for name in (DP_PARTS[1], DP_PARTS[0], DP_PARTS[2]):
            values = ring_gather(values, name)
        blocks = values.reshape(sizes[2], sizes[0], sizes[1], -1, values.shape[-1])
        return blocks.transpose(1, 2, 0, 3, 4).reshape(values.shape)

    rest = jnp.concatenate(
        [
            attention_out[3],
            expert_out[3].transpose(1, 0, 2).reshape(re, n_e * e_cols),
            routing_out[3].T,
        ],
        axis=1,
    )
    rest = gather(rest)
    attention_served = rest[:, :cols]
    expert_served = (
        rest[:, cols : cols + n_e * e_cols].reshape(e_rows, n_e, e_cols).transpose(1, 0, 2)
    )
    routing_served = rest[:, cols + n_e * e_cols :].T
    return (
        attention_out[0],
        attention_out[1],
        attention_out[2],
        attention_served,
        expert_out[0],
        expert_out[1],
        expert_out[2],
        expert_served,
        mine(routing_out[0]),
        mine(routing_out[1]),
        mine(routing_out[2]),
        routing_served,
    )


def split_mesh(mesh):
    column = mesh.devices[:, 0]
    sizes = (
        len({d.coords[0] for d in column}),
        len({d.coords[2] for d in column}),
        len({d.core_on_chip for d in column}),
    )
    devices = mesh.devices.reshape(sizes + mesh.devices.shape[1:])
    return Mesh(devices, DP_PARTS + ("tensor",))


def solution(mesh):
    mesh = split_mesh(mesh)
    in_specs = (
        P(DP, None, None, "tensor"),
        P(DP, None, None, None, "tensor"),
        P(DP, "tensor", None, None, None),
        P(DP, "tensor"),
        P(DP, "tensor"),
        P(DP, "tensor"),
        P(None, DP, "tensor"),
        P(None, DP, "tensor"),
        P(None, DP, "tensor"),
        P(None, (DP + ("tensor",))),
        P(None, (DP + ("tensor",))),
        P(None, (DP + ("tensor",))),
        P(),
        P(),
        P(),
    )
    out_specs = (
        P(DP, "tensor"),
        P(DP, "tensor"),
        P(DP, "tensor"),
        P(None, "tensor"),
        P(None, DP, "tensor"),
        P(None, DP, "tensor"),
        P(None, DP, "tensor"),
        P(None, None, "tensor"),
        P(None, (DP + ("tensor",))),
        P(None, (DP + ("tensor",))),
        P(None, (DP + ("tensor",))),
        P(),
    )
    return jax.shard_map(local, mesh=mesh, in_specs=in_specs, out_specs=out_specs, check_vma=False)
```

```python
import jax
import jax.numpy as jnp
from jax import lax
from jax.sharding import Mesh, PartitionSpec as P

EXPERTS = 32

PARAMS = 5261312


BETA_ONE = 0.9
BETA_TWO = 0.999
EPSILON = 1e-08
DECAY = 0.1

DP_PARTS = ("dp_x", "dp_z", "dp_core")
DP = DP_PARTS


def adam_update(grad_sum, master, first, second, clip, rate, first_fix, second_fix, mask):
    grad = clip * grad_sum
    momentum = BETA_ONE * first + (1.0 - BETA_ONE) * grad
    variance = BETA_TWO * second + (1.0 - BETA_TWO) * grad * grad
    update = (
        momentum / first_fix / (jnp.sqrt(variance / second_fix) + EPSILON) + DECAY * mask * master
    )
    renewed = master - rate * update
    return (renewed, momentum, variance, renewed.astype(jnp.bfloat16))


def ring_sum(values, name):
    size = lax.axis_size(name)
    ring = [values] + [
        lax.ppermute(values, name, [(i, (i + size - k) % size) for i in range(size)])
        for k in range(1, size)
    ]
    ring = jnp.roll(jnp.stack(ring), lax.axis_index(name), axis=0)
    return jnp.sum(ring, axis=0)


def local(
    attention_grads,
    expert_grads,
    routing_grads,
    attention_master,
    attention_first,
    attention_second,
    expert_master,
    expert_first,
    expert_second,
    routing_master,
    routing_first,
    routing_second,
    step_count,
    learn_rate,
    clip_level,
):
    n_dp = lax.axis_size(DP)
    n_t = lax.axis_size("tensor")
    t_idx = lax.axis_index("tensor")

    att = attention_grads[0, 0]
    exp = expert_grads[0, 0]
    rte = routing_grads[0, 0, 0]
    rows, cols = att.shape
    n_e, e_rows, e_cols = exp.shape
    n_r, r_cols = rte.shape
    ra = rows // n_dp
    re = e_rows // n_dp
    rc = r_cols // n_dp
    own = rc // n_t

    exp_rows = exp.transpose(1, 0, 2).reshape(e_rows, n_e * e_cols)
    send = jnp.concatenate([att, exp_rows, rte.T], axis=1)
    got = lax.all_to_all(send, DP, 0, 0, tiled=True)
    total = jnp.sum(got.reshape(n_dp, ra, -1).astype(jnp.float32), axis=0)
    attention_sum = total[:, :cols]
    expert_sum = total[:, cols : cols + n_e * e_cols].reshape(re, n_e, e_cols).transpose(1, 0, 2)
    route_part = total[:, cols + n_e * e_cols :].T

    local_squares = jnp.sum(attention_sum * attention_sum) + jnp.sum(expert_sum * expert_sum)
    slot = (jnp.arange(rc) // own == t_idx)[None, :]

    def placed(values):
        return jnp.where(slot, jnp.tile(values, (1, n_t)), 0.0)

    packed = jnp.stack(
        [
            route_part,
            placed(routing_master),
            placed(routing_first),
            placed(routing_second),
            jnp.full((n_r, rc), 0.0).at[0, 0].set(local_squares),
        ]
    )
    packed = ring_sum(packed, "tensor")
    route_sum = packed[0]
    route_master_blk, route_first_blk, route_second_blk = packed[1], packed[2], packed[3]
    group_squares = packed[4, 0, 0] + jnp.sum(route_sum * route_sum)

    squares = group_squares
    for name in DP_PARTS[::-1]:
        squares = ring_sum(squares, name)

    grad_norm = jnp.sqrt(squares)
    clip = jnp.minimum(1.0, clip_level[0] * jnp.sqrt(jnp.float32(PARAMS)) / (grad_norm + 1e-06))
    steps_done = step_count[0].astype(jnp.float32)
    first_fix = 1.0 - jnp.power(jnp.float32(BETA_ONE), steps_done)
    second_fix = 1.0 - jnp.power(jnp.float32(BETA_TWO), steps_done)
    rate = learn_rate[0]
    one = jnp.float32(1.0)
    attention_out = adam_update(
        attention_sum, attention_master, attention_first, attention_second,
        clip, rate, first_fix, second_fix, one,
    )
    expert_out = adam_update(
        expert_sum, expert_master, expert_first, expert_second,
        clip, rate, first_fix, second_fix, one,
    )
    row_index = jnp.arange(n_r, dtype=jnp.int32)
    routing_mask = (row_index < EXPERTS).astype(jnp.float32)[:, None]
    routing_out = adam_update(
        route_sum, route_master_blk, route_first_blk, route_second_blk,
        clip, rate, first_fix, second_fix, routing_mask,
    )

    def mine(values):
        return lax.dynamic_slice_in_dim(values, t_idx * own, own, axis=1)

    def ring_gather(values, name):
        size = lax.axis_size(name)
        ring = [values] + [
            lax.ppermute(values, name, [(i, (i + size - k) % size) for i in range(size)])
            for k in range(1, size)
        ]
        stacked = jnp.stack(ring)
        stacked = jnp.roll(stacked, lax.axis_index(name), axis=0)
        return stacked.reshape((-1,) + values.shape[1:])

    def gather(values):
        sizes = [lax.axis_size(name) for name in DP_PARTS]
        for name in (DP_PARTS[1], DP_PARTS[0], DP_PARTS[2]):
            values = ring_gather(values, name)
        blocks = values.reshape(sizes[2], sizes[0], sizes[1], -1, values.shape[-1])
        return blocks.transpose(1, 2, 0, 3, 4).reshape(values.shape)

    rest = jnp.concatenate(
        [
            attention_out[3],
            expert_out[3].transpose(1, 0, 2).reshape(re, n_e * e_cols),
            routing_out[3].T,
        ],
        axis=1,
    )
    rest = gather(rest)
    attention_served = rest[:, :cols]
    expert_served = (
        rest[:, cols : cols + n_e * e_cols].reshape(e_rows, n_e, e_cols).transpose(1, 0, 2)
    )
    routing_served = rest[:, cols + n_e * e_cols :].T
    return (
        attention_out[0],
        attention_out[1],
        attention_out[2],
        attention_served,
        expert_out[0],
        expert_out[1],
        expert_out[2],
        expert_served,
        mine(routing_out[0]),
        mine(routing_out[1]),
        mine(routing_out[2]),
        routing_served,
    )


def split_mesh(mesh):
    column = mesh.devices[:, 0]
    sizes = (
        len({d.coords[0] for d in column}),
        len({d.coords[2] for d in column}),
        len({d.core_on_chip for d in column}),
    )
    devices = mesh.devices.reshape(sizes + mesh.devices.shape[1:])
    return Mesh(devices, DP_PARTS + ("tensor",))


def solution(mesh):
    mesh = split_mesh(mesh)
    in_specs = (
        P(DP, None, None, "tensor"),
        P(DP, None, None, None, "tensor"),
        P(DP, "tensor", None, None, None),
        P(DP, "tensor"),
        P(DP, "tensor"),
        P(DP, "tensor"),
        P(None, DP, "tensor"),
        P(None, DP, "tensor"),
        P(None, DP, "tensor"),
        P(None, (DP + ("tensor",))),
        P(None, (DP + ("tensor",))),
        P(None, (DP + ("tensor",))),
        P(),
        P(),
        P(),
    )
    out_specs = (
        P(DP, "tensor"),
        P(DP, "tensor"),
        P(DP, "tensor"),
        P(None, "tensor"),
        P(None, DP, "tensor"),
        P(None, DP, "tensor"),
        P(None, DP, "tensor"),
        P(None, None, "tensor"),
        P(None, (DP + ("tensor",))),
        P(None, (DP + ("tensor",))),
        P(None, (DP + ("tensor",))),
        P(),
    )
    return jax.shard_map(local, mesh=mesh, in_specs=in_specs, out_specs=out_specs, check_vma=False)
```
